512 devices in a mesh: seq: 256 (over y_hi, z, x, core), dp: 2 (over y_lo).
Axes of the slice: x: 4, y: 8 (y_hi: 4, y_lo: 2; y = y_hi * 2 + y_lo), z: 8, core: 2. Of those that a mesh axis runs over, the one named last changes fastest.
Arguments:
- q_raw: bfloat16 [2, 32768, 2560], P('dp', 'seq'), may hold values from -33000 to 33000
- k_raw: bfloat16 [2, 32768, 2560], P('dp', 'seq'), may hold values from -19000 to 19000
- values: bfloat16 [2, 32768, 2560], P('dp', 'seq'), may hold values from -6 to 6
- cotangent: bfloat16 [2, 32768, 2560], P('dp', 'seq'), may hold values from -6 to 6
- q_gain: float32 [2560], replicated, may hold values from 0.5 to 1.5
- k_gain: float32 [2560], replicated, may hold values from 0.5 to 1.5
- key_tiles: int32 [256, 4], P('seq'), may hold values from -1 to 255, as said below
Outputs:
- q_grad: bfloat16 [2, 32768, 2560], P('dp', 'seq')
- k_grad: bfloat16 [2, 32768, 2560], P('dp', 'seq')
- v_grad: bfloat16 [2, 32768, 2560], P('dp', 'seq')
- q_gain_grad: float32 [2560], replicated
- k_gain_grad: float32 [2560], replicated
The draws below stay inside these ranges and needn't reach their ends.
Inputs may be any that keep to these rules, and one draw needn't show every extreme that they name: `key_tiles`: row a, column 2 j + s (j below 2, s 0 or 1) holds -1 or the tile a - 2^j (s = 0) or a + 2^j (s = 1); it is -1 wherever that tile lies outside the clip.
All inputs are finite; a program needn't handle non-finite values.
Results may differ from the reference program's by a relative error of at most 0.013.
The reference program's roundings to bfloat16 on the way (of `prob` and `score_grad`) count: a program that leaves them out, or rounds other values in their place, can miss the bound.
Values may be sent and summed in bfloat16 or wider, within the bound.
No kernel may reach another device: no remote copies, remote signals or barrier semaphores. Data moves between devices by JAX's collectives and lax.ppermute only.
A program may use at most 128 MiB of HBM per device.

```python
import math
import jax
import jax.numpy as jnp
from jax import lax

HEADS = 20
HEAD = 128
TOK_DEV = 128
LEVELS = 2
FEAT = 2560
TILES = 256
TOKENS = 32768
REPLICAS = 2


def projections(key):
    shape = (REPLICAS, TOKENS, FEAT)
    upper = math.log(10.0)
    k_base = jnp.clip(jax.random.normal(jax.random.fold_in(key, 11), shape, jnp.float32), -4.0, 4.0)
    q_base = jnp.clip(jax.random.normal(jax.random.fold_in(key, 12), shape, jnp.float32), -4.0, 4.0)
    k_cols = jnp.exp(jax.random.uniform(jax.random.fold_in(key, 13), (FEAT,), jnp.float32, 0.0, upper))
    q_cols = jnp.exp(jax.random.uniform(jax.random.fold_in(key, 14), (FEAT,), jnp.float32, 0.0, upper))
    k_rows = jnp.exp(jax.random.uniform(jax.random.fold_in(key, 15), (REPLICAS, TOKENS, 1), jnp.float32, 0.0, upper))
    q_rows = jnp.exp(jax.random.uniform(jax.random.fold_in(key, 16), (REPLICAS, TOKENS, 1), jnp.float32, 0.0, upper))
    k_scales = k_cols * k_rows
    k_full = k_base * k_scales
    q_full = q_base * q_cols * q_rows
    return (q_full, k_full)


def draw_q_raw(key, part):
    return projections(key)[0].astype(jnp.bfloat16)


def draw_k_raw(key, part):
    return projections(key)[1].astype(jnp.bfloat16)


def draw_key_tiles(key, part):
    tiles = jnp.arange(TILES, dtype=jnp.int32)[:, None]
    columns = jnp.arange(2 * LEVELS, dtype=jnp.int32)[None, :]
    levels = columns // 2
    signs = 2 * (columns % 2) - 1
    target = tiles + signs * jnp.left_shift(jnp.ones_like(levels), levels)
    draws = jax.random.randint(key, (TILES, 2 * LEVELS), 0, 8, dtype=jnp.int32)
    kept = draws < 6 - 2 * levels
    inside = (target >= 0) & (target < TILES)
    return jnp.where(kept & inside, target, -1).astype(jnp.int32)


def shard_levels(key, dims, shards, smallest, largest):
    factor_of = 1.0
    for position, parts in shards:
        heights = jax.random.uniform(jax.random.fold_in(jax.random.fold_in(key, 6), position), (parts,), jnp.float32, smallest / len(shards), largest / len(shards))
        factor_of = factor_of * jnp.repeat(jnp.exp(heights), dims[position] // parts).reshape((-1,) + (1,) * (len(dims) - 1 - position))
    return factor_of


def normal_values(key, dims, scale, bound, split=(), kind=jnp.bfloat16):
    level = shard_levels(key, dims, split, -0.22, 0.18) if split else 1.0
    values = jax.random.normal(key, dims, jnp.float32) * scale * level
    return jnp.minimum(jnp.maximum(values, -bound), bound).astype(kind)


def setup_inputs(seed: int = 0) -> dict:
    key_list = jax.random.split(jax.random.key(seed), 8)
    return {
        "q_raw": draw_q_raw(jax.random.fold_in(key_list[7], 71), 0),
        "k_raw": draw_k_raw(jax.random.fold_in(key_list[7], 71), 0),
        "values": normal_values(key_list[2], (REPLICAS, TOKENS, FEAT), 1.0, 6.0, ((0, 2), (1, 256))),
        "cotangent": normal_values(key_list[3], (REPLICAS, TOKENS, FEAT), 1.0, 6.0, ((0, 2), (1, 256))),
        "q_gain": jnp.clip(1.0 + 0.1 * jax.random.normal(key_list[4], (FEAT,), jnp.float32), 0.5, 1.5),
        "k_gain": jnp.clip(1.0 + 0.1 * jax.random.normal(key_list[5], (FEAT,), jnp.float32), 0.5, 1.5),
        "key_tiles": draw_key_tiles(jax.random.fold_in(key_list[7], 71), 0),
    }


EPS = 1e-06

def level_offsets():
    return [sign * 2 ** level for level in range(LEVELS) for sign in (-1, 1)]

def to_single(array):
    return array.astype(jnp.float32)

def normalize(raw):
    numbers = raw.astype(jnp.float32)
    inverse = lax.rsqrt(lax.optimization_barrier(jnp.mean(numbers * numbers, axis=-1, keepdims=True)) + EPS)
    return (numbers * inverse, inverse)

def norm_backward(grad_norm, gain, hat, inverse):
    scaled = grad_norm * gain
    inner = lax.optimization_barrier(jnp.mean(scaled * hat, axis=-1, keepdims=True))
    return (inverse * (scaled - hat * inner), lax.optimization_barrier(jnp.sum(grad_norm * hat, axis=0)))

def query_side(q_tile, key_block, value_block, grad_out, live, scale):
    scores = jnp.einsum('qhd,khd->hqk', to_single(q_tile), to_single(key_block)) * scale
    masked = jnp.where(live, scores, -jnp.inf)
    highest = lax.optimization_barrier(jnp.max(masked, axis=-1, keepdims=True))
    total = lax.optimization_barrier(jnp.sum(jnp.exp(masked - highest), axis=-1, keepdims=True))
    log_total = highest + jnp.log(total)
    prob = jnp.where(live, jnp.exp(scores - log_total), 0.0).astype(jnp.bfloat16)
    attended = jnp.einsum('hqk,khd->qhd', to_single(prob), to_single(value_block))
    delta = jnp.transpose(lax.optimization_barrier(jnp.sum(to_single(grad_out) * attended, axis=-1)))[:, :, None]
    prob_grad = jnp.einsum('qhd,khd->hqk', to_single(grad_out), to_single(value_block))
    score_grad = (to_single(prob) * (prob_grad - delta) * scale).astype(jnp.bfloat16)
    grad_q = jnp.einsum('hqk,khd->qhd', to_single(score_grad), to_single(key_block))
    return (grad_q, log_total, delta)

def key_side(q_tile, grad_out, log_total, delta, key_tile, value_tile, keep, scale):
    scores = jnp.einsum('qhd,khd->hqk', to_single(q_tile), to_single(key_tile)) * scale
    prob = jnp.where(keep, jnp.exp(scores - log_total), 0.0).astype(jnp.bfloat16)
    prob_grad = jnp.einsum('qhd,khd->hqk', to_single(grad_out), to_single(value_tile))
    score_grad = (to_single(prob) * (prob_grad - delta) * scale).astype(jnp.bfloat16)
    grad_k = jnp.einsum('hqk,qhd->khd', to_single(score_grad), to_single(q_tile))
    grad_v = jnp.einsum('hqk,qhd->khd', to_single(prob), to_single(grad_out))
    return (grad_k, grad_v)

def rounded_part(part):
    return lax.optimization_barrier(part.astype(jnp.bfloat16)).astype(jnp.float32)

def reference(q_raw, k_raw, values, cotangent, q_gain, k_gain, key_tiles):
    scale = 1.0 / math.sqrt(HEAD)
    offsets = jnp.array(level_offsets(), dtype=jnp.int32)
    slots = 2 * LEVELS
    tile_ids = jnp.arange(TILES, dtype=jnp.int32)
    q_grads = []
    k_grads = []
    v_grads = []
    q_gain_grad = jnp.zeros((FEAT,), jnp.float32)
    k_gain_grad = jnp.zeros((FEAT,), jnp.float32)
    for replica in range(REPLICAS):
        q_hat, q_inv = normalize(q_raw[replica])
        k_hat, k_inv = normalize(k_raw[replica])
        q_norm = (q_hat * q_gain).astype(jnp.bfloat16).reshape(TILES, TOK_DEV, HEADS, HEAD)
        k_norm = (k_hat * k_gain).astype(jnp.bfloat16).reshape(TILES, TOK_DEV, HEADS, HEAD)
        value_rows = values[replica].reshape(TILES, TOK_DEV, HEADS, HEAD)
        grad_rows = cotangent[replica].reshape(TILES, TOK_DEV, HEADS, HEAD)

        def forward(tile):
            nearby = jnp.concatenate([tile[None], jnp.clip(tile + offsets, 0, TILES - 1)]).astype(jnp.int32)
            key_block = jnp.take(k_norm, nearby, axis=0).reshape(-1, HEADS, HEAD)
            value_block = jnp.take(value_rows, nearby, axis=0).reshape(-1, HEADS, HEAD)
            live = jnp.repeat(jnp.concatenate([jnp.ones((1,), bool), key_tiles[tile] >= 0]), TOK_DEV)
            return query_side(q_norm[tile], key_block, value_block, grad_rows[tile], live, scale)
        grad_q, log_total, delta = lax.map(forward, tile_ids)

        def backward(tile):
            source = tile - offsets
            valid = (source >= 0) & (source < TILES)
            clipped = jnp.clip(source, 0, TILES - 1).astype(jnp.int32)
            total_k, total_v = key_side(q_norm[tile], grad_rows[tile], log_total[tile], delta[tile], k_norm[tile], value_rows[tile], True, scale)
            for slot in range(slots):
                root = clipped[slot]
                keep = valid[slot] & (key_tiles[root, slot] >= 0)
                part_k, part_v = key_side(q_norm[root], grad_rows[root], log_total[root], delta[root], k_norm[tile], value_rows[tile], keep, scale)
                total_k = total_k + rounded_part(part_k)
                total_v = total_v + rounded_part(part_v)
            return (total_k, total_v)
        grad_k, grad_v = lax.map(backward, tile_ids)
        q_norm_grad = grad_q.reshape(TOKENS, FEAT)
        k_norm_grad = grad_k.reshape(TOKENS, FEAT)
        v_sum = grad_v.reshape(TOKENS, FEAT)
        q_back, q_part = norm_backward(q_norm_grad, q_gain, q_hat, q_inv)
        k_back, k_part = norm_backward(k_norm_grad, k_gain, k_hat, k_inv)
        q_grads.append(q_back.astype(jnp.bfloat16))
        k_grads.append(k_back.astype(jnp.bfloat16))
        v_grads.append(v_sum.astype(jnp.bfloat16))
        q_gain_grad = q_gain_grad + q_part
        k_gain_grad = k_gain_grad + k_part
    return (jnp.stack(q_grads), jnp.stack(k_grads), jnp.stack(v_grads), q_gain_grad, k_gain_grad)
```

```python
import math

import jax
import jax.numpy as jnp
from jax import lax
from jax.sharding import PartitionSpec as P

HEAD = 128
LEVELS = 2


EPS = 1e-06


def from_behind(value, axis, steps):
    count = lax.axis_size(axis)
    first, last = (max(0, -steps), min(count, count - steps))
    return lax.ppermute(value, axis, [(source, source + steps) for source in range(first, last)])


def all_sum(value, axes):
    for axis in axes:
        count = lax.axis_size(axis)
        bit = 1
        while bit < count:
            value = value + lax.ppermute(value, axis, [(i, i ^ bit) for i in range(count)])
            bit *= 2
    return value


def level_offsets(levels):
    return [sign * 2**level for level in range(levels) for sign in (-1, 1)]


def normalize(raw):
    numbers = raw.astype(jnp.float32)
    inverse = lax.rsqrt(jnp.mean(numbers * numbers, axis=-1, keepdims=True) + EPS)
    return (numbers * inverse, inverse)


def norm_backward(grad_norm, gain, hat, inverse):
    scaled = grad_norm * gain
    inner = jnp.mean(scaled * hat, axis=-1, keepdims=True)
    return (inverse * (scaled - hat * inner), jnp.sum(grad_norm * hat, axis=0))


def head_slice(array, index, group_width):
    return lax.dynamic_slice_in_dim(array, index * group_width, group_width, 1)


def heads_last(block):
    moved = jnp.transpose(block, (1, 0, 2, 3))
    return moved.reshape(moved.shape[0], -1)


def body(q_raw, k_raw, values, cotangent, q_gain, k_gain, key_tiles):
    tile_rows = q_raw.shape[1]
    features = q_raw.shape[2]
    heads = features // HEAD
    group_width = 4
    groups = heads // group_width
    scale = 1.0 / math.sqrt(HEAD)
    offsets = level_offsets(LEVELS)
    slots = len(offsets)
    q_hat, q_inv = normalize(q_raw[0])
    k_hat, k_inv = normalize(k_raw[0])
    q_norm = (q_hat * q_gain).astype(jnp.bfloat16).reshape(tile_rows, heads, HEAD)
    k_norm = (k_hat * k_gain).astype(jnp.bfloat16).reshape(tile_rows, heads, HEAD)
    value_rows = values[0].reshape(tile_rows, heads, HEAD)
    grad_rows = cotangent[0].reshape(tile_rows, heads, HEAD)
    entries = key_tiles[0]
    fetched = [from_behind((k_norm, value_rows), "seq", -offset) for offset in offsets]
    key_block = jnp.concatenate([k_norm] + [pair[0] for pair in fetched], axis=0)
    value_block = jnp.concatenate([value_rows] + [pair[1] for pair in fetched], axis=0)
    live = jnp.repeat(jnp.concatenate([jnp.ones((1,), bool), entries >= 0]), tile_rows)

    def attend(index):
        q_group = head_slice(q_norm, index, group_width)
        k_group = head_slice(key_block, index, group_width)
        v_group = head_slice(value_block, index, group_width)
        g_group = head_slice(grad_rows, index, group_width)
        scores = (
            jnp.einsum("qhd,khd->hqk", q_group, k_group, preferred_element_type=jnp.float32) * scale
        )
        highest = jnp.max(jnp.where(live, scores, -jnp.inf), axis=-1)
        total = jnp.sum(jnp.where(live, jnp.exp(scores - highest[:, :, None]), 0.0), axis=-1)
        log_total = highest + jnp.log(total)
        prob = jnp.where(live, jnp.exp(scores - log_total[:, :, None]), 0.0).astype(jnp.bfloat16)
        attended = jnp.einsum("hqk,khd->qhd", prob, v_group, preferred_element_type=jnp.float32)
        delta = jnp.transpose(jnp.sum(g_group.astype(jnp.float32) * attended, axis=-1))
        prob_grad = jnp.einsum("qhd,khd->hqk", g_group, v_group, preferred_element_type=jnp.float32)
        score_grad = (prob.astype(jnp.float32) * (prob_grad - delta[:, :, None]) * scale).astype(
            jnp.bfloat16
        )
        grad_q = jnp.einsum("hqk,khd->qhd", score_grad, k_group, preferred_element_type=jnp.float32)
        grad_k = jnp.einsum("hqk,qhd->khd", score_grad, q_group, preferred_element_type=jnp.float32)
        grad_v = jnp.einsum("hqk,qhd->khd", prob, g_group, preferred_element_type=jnp.float32)
        return (
            grad_q,
            grad_k[:tile_rows],
            grad_v[:tile_rows],
            grad_k[tile_rows:].astype(jnp.bfloat16),
            grad_v[tile_rows:].astype(jnp.bfloat16),
            log_total,
            delta,
        )

    results = lax.map(attend, jnp.arange(groups, dtype=jnp.int32))
    q_norm_grad = heads_last(results[0])
    k_norm_grad = heads_last(results[1])
    v_sum = heads_last(results[2])
    far_k = jnp.transpose(
        results[3].reshape(groups, slots, tile_rows, group_width, HEAD), (1, 2, 0, 3, 4)
    )
    far_v = jnp.transpose(
        results[4].reshape(groups, slots, tile_rows, group_width, HEAD), (1, 2, 0, 3, 4)
    )
    far_k = far_k.reshape(slots, tile_rows, features)
    far_v = far_v.reshape(slots, tile_rows, features)
    for slot in range(slots):
        back_k, back_v = from_behind((far_k[slot], far_v[slot]), "seq", offsets[slot])
        k_norm_grad = k_norm_grad + back_k.astype(jnp.float32)
        v_sum = v_sum + back_v.astype(jnp.float32)
    q_back, q_part = norm_backward(q_norm_grad, q_gain, q_hat, q_inv)
    k_back, k_part = norm_backward(k_norm_grad, k_gain, k_hat, k_inv)
    gain_grads = all_sum(jnp.concatenate([q_part, k_part]), ("dp", "seq"))
    q_gain_grad, k_gain_grad = gain_grads[:features], gain_grads[features:]
    return (
        q_back.astype(jnp.bfloat16)[None],
        k_back.astype(jnp.bfloat16)[None],
        v_sum.astype(jnp.bfloat16)[None],
        q_gain_grad,
        k_gain_grad,
    )


def solution(mesh):
    return jax.shard_map(
        body,
        mesh=mesh,
        in_specs=(
            P("dp", "seq", None),
            P("dp", "seq", None),
            P("dp", "seq", None),
            P("dp", "seq", None),
            P(),
            P(),
            P("seq", None),
        ),
        out_specs=(P("dp", "seq", None), P("dp", "seq", None), P("dp", "seq", None), P(), P()),
        check_vma=False,
    )
```

```python
import functools
import math

import jax
import jax.numpy as jnp
from jax import lax
from jax.experimental import pallas as pl
from jax.experimental.pallas import tpu as pltpu
from jax.sharding import PartitionSpec as P

HEAD = 128
LEVELS = 2
HEADS_PER_STEP = 4


EPS = 1e-06

NT = (((1,), (1,)), ((), ()))
TN = (((0,), (0,)), ((), ()))


def from_behind(value, axis, steps):
    count = lax.axis_size(axis)
    first, last = (max(0, -steps), min(count, count - steps))
    return lax.ppermute(value, axis, [(source, source + steps) for source in range(first, last)])


def all_sum(value, axes):
    for axis in axes:
        count = lax.axis_size(axis)
        bit = 1
        while bit < count:
            value = value + lax.ppermute(value, axis, [(i, i ^ bit) for i in range(count)])
            bit *= 2
    return value


def level_offsets(levels):
    return [sign * 2**level for level in range(levels) for sign in (-1, 1)]


def normalize(raw):
    numbers = raw.astype(jnp.float32)
    inverse = lax.rsqrt(jnp.mean(numbers * numbers, axis=-1, keepdims=True) + EPS)
    return (numbers * inverse, inverse)


def norm_backward(grad_norm, gain, hat, inverse):
    scaled = grad_norm * gain
    inner = jnp.mean(scaled * hat, axis=-1, keepdims=True)
    return (inverse * (scaled - hat * inner), jnp.sum(grad_norm * hat, axis=0))


def attention_kernel(live_ref, q_ref, k_ref, v_ref, g_ref, *refs):
    slots = (len(refs) - 3) // 2
    fetched = refs[:slots]
    dq_ref, dk_ref, dv_ref = refs[slots:slots + 3]
    far = refs[slots + 3:]
    rows = q_ref.shape[0]
    scale = 1.0 / math.sqrt(HEAD)
    live = live_ref[...] > 0
    for h in range(q_ref.shape[1] // HEAD):
        cols = pl.ds(h * HEAD, HEAD)
        q = q_ref[:, cols]
        g = g_ref[:, cols]
        keys = jnp.concatenate([k_ref[:, cols]] + [r[0, :, cols] for r in fetched], axis=0)
        vals = jnp.concatenate([v_ref[:, cols]] + [r[1, :, cols] for r in fetched], axis=0)
        scores = lax.dot_general(q, keys, NT, preferred_element_type=jnp.float32) * scale
        highest = jnp.max(jnp.where(live, scores, -jnp.inf), axis=1, keepdims=True)
        total = jnp.sum(jnp.where(live, jnp.exp(scores - highest), 0.0), axis=1, keepdims=True)
        log_total = highest + jnp.log(total)
        prob = jnp.where(live, jnp.exp(scores - log_total), 0.0).astype(jnp.bfloat16)
        attended = jnp.dot(prob, vals, preferred_element_type=jnp.float32)
        delta = jnp.sum(g.astype(jnp.float32) * attended, axis=1, keepdims=True)
        prob_grad = lax.dot_general(g, vals, NT, preferred_element_type=jnp.float32)
        score_grad = (prob.astype(jnp.float32) * (prob_grad - delta) * scale).astype(jnp.bfloat16)
        dq_ref[:, cols] = jnp.dot(score_grad, keys, preferred_element_type=jnp.float32)
        grad_k = lax.dot_general(score_grad, q, TN, preferred_element_type=jnp.float32)
        grad_v = lax.dot_general(prob, g, TN, preferred_element_type=jnp.float32)
        dk_ref[:, cols] = grad_k[:rows]
        dv_ref[:, cols] = grad_v[:rows]
        for slot in range(slots):
            part = slice((slot + 1) * rows, (slot + 2) * rows)
            far[slot][0, :, cols] = grad_k[part].astype(jnp.bfloat16)
            far[slot][1, :, cols] = grad_v[part].astype(jnp.bfloat16)


def attention(live, q_norm, k_norm, value_rows, grad_rows, fetched):
    rows, features = q_norm.shape
    width = HEADS_PER_STEP * HEAD
    slots = len(fetched)
    tile = pl.BlockSpec((rows, width), lambda h: (0, h))
    pair = pl.BlockSpec((2, rows, width), lambda h: (0, 0, h))
    f32 = jax.ShapeDtypeStruct((rows, features), jnp.float32)
    bf16_pair = jax.ShapeDtypeStruct((2, rows, features), jnp.bfloat16)
    keys = rows * (slots + 1)
    flops = 2 * rows * keys * features * 6
    return pl.pallas_call(
        attention_kernel,
        grid=(features // width,),
        in_specs=[pl.BlockSpec(live.shape, lambda h: (0, 0))] + [tile] * 4 + [pair] * slots,
        out_specs=[tile] * 3 + [pair] * slots,
        out_shape=[f32] * 3 + [bf16_pair] * slots,
        cost_estimate=pl.CostEstimate(
            flops=flops,
            transcendentals=2 * rows * keys * (features // HEAD),
            bytes_accessed=2 * rows * features * (4 + 4 * slots) + 12 * rows * features,
        ),
    )(live, q_norm, k_norm, value_rows, grad_rows, *fetched)


def body(q_raw, k_raw, values, cotangent, q_gain, k_gain, key_tiles):
    tile_rows = q_raw.shape[1]
    features = q_raw.shape[2]
    offsets = level_offsets(LEVELS)
    q_hat, q_inv = normalize(q_raw[0])
    k_hat, k_inv = normalize(k_raw[0])
    q_norm = (q_hat * q_gain).astype(jnp.bfloat16)
    k_norm = (k_hat * k_gain).astype(jnp.bfloat16)
    value_rows = values[0]
    grad_rows = cotangent[0]
    entries = key_tiles[0]
    stacked = jnp.stack([k_norm, value_rows])
    fetched = [from_behind(stacked, "seq", -offset) for offset in offsets]
    live = jnp.repeat(
        jnp.concatenate([jnp.ones((1,), jnp.int32), (entries >= 0).astype(jnp.int32)]), tile_rows
    )[None, :]
    q_norm_grad, k_norm_grad, v_sum, *far = attention(
        live, q_norm, k_norm, value_rows, grad_rows, fetched
    )
    for slot, offset in enumerate(offsets):
        back = from_behind(far[slot], "seq", offset)
        k_norm_grad = k_norm_grad + back[0].astype(jnp.float32)
        v_sum = v_sum + back[1].astype(jnp.float32)
    q_back, q_part = norm_backward(q_norm_grad, q_gain, q_hat, q_inv)
    k_back, k_part = norm_backward(k_norm_grad, k_gain, k_hat, k_inv)
    gain_grads = all_sum(jnp.concatenate([q_part, k_part]), ("dp", "seq"))
    q_gain_grad, k_gain_grad = gain_grads[:features], gain_grads[features:]
    return (
        q_back.astype(jnp.bfloat16)[None],
        k_back.astype(jnp.bfloat16)[None],
        v_sum.astype(jnp.bfloat16)[None],
        q_gain_grad,
        k_gain_grad,
    )


def solution(mesh):
    return jax.shard_map(
        body,
        mesh=mesh,
        in_specs=(
            P("dp", "seq", None),
            P("dp", "seq", None),
            P("dp", "seq", None),
            P("dp", "seq", None),
            P(),
            P(),
            P("seq", None),
        ),
        out_specs=(P("dp", "seq", None), P("dp", "seq", None), P("dp", "seq", None), P(), P()),
        check_vma=False,
    )
```

```python
import functools
import math

import jax
import jax.numpy as jnp
from jax import lax
from jax.experimental import pallas as pl
from jax.experimental.pallas import tpu as pltpu
from jax.sharding import PartitionSpec as P

HEAD = 128
LEVELS = 2
HEADS_PER_STEP = 4


EPS = 1e-06

NT = (((1,), (1,)), ((), ()))
TN = (((0,), (0,)), ((), ()))


def from_behind(value, axis, steps):
    count = lax.axis_size(axis)
    first, last = (max(0, -steps), min(count, count - steps))
    return lax.ppermute(value, axis, [(source, source + steps) for source in range(first, last)])


def pairs_permute(value, axis, pairs):
    count = lax.axis_size(axis)
    return lax.ppermute(value, axis, [(i, j) for i, j in pairs if 0 <= j < count])


def fetch_neighbours(value, axis):
    count = lax.axis_size(axis)
    behind = from_behind(value, axis, 1)
    ahead = from_behind(value, axis, -1)
    far_behind = pairs_permute(value, axis, [(i, i + 2) for i in range(0, count, 2)])
    far_ahead = pairs_permute(value, axis, [(i, i - 2) for i in range(1, count, 2)])
    relay_behind = pairs_permute(behind, axis, [(i, i + 1) for i in range(0, count, 2)])
    relay_ahead = pairs_permute(ahead, axis, [(i, i - 1) for i in range(1, count, 2)])
    odd = lax.axis_index(axis) % 2 == 1
    return [
        behind,
        ahead,
        jnp.where(odd, relay_behind, far_behind),
        jnp.where(odd, far_ahead, relay_ahead),
    ]


def all_sum(value, axes):
    for axis in axes:
        count = lax.axis_size(axis)
        bit = 1
        while bit < count:
            value = value + lax.ppermute(value, axis, [(i, i ^ bit) for i in range(count)])
            bit *= 2
    return value


def level_offsets(levels):
    return [sign * 2**level for level in range(levels) for sign in (-1, 1)]


def normalize(raw):
    numbers = raw.astype(jnp.float32)
    inverse = lax.rsqrt(jnp.mean(numbers * numbers, axis=-1, keepdims=True) + EPS)
    return (numbers * inverse, inverse)


def norm_backward(grad_norm, gain, hat, inverse):
    scaled = grad_norm * gain
    inner = jnp.mean(scaled * hat, axis=-1, keepdims=True)
    return (inverse * (scaled - hat * inner), jnp.sum(grad_norm * hat, axis=0))


def attention_kernel(live_ref, q_ref, k_ref, v_ref, g_ref, *refs):
    slots = (len(refs) - 3) // 2
    fetched = refs[:slots]
    dq_ref, dk_ref, dv_ref = refs[slots:slots + 3]
    far = refs[slots + 3:]
    rows = q_ref.shape[0]
    scale = 1.0 / math.sqrt(HEAD)
    live = live_ref[...] > 0
    for h in range(q_ref.shape[1] // HEAD):
        cols = pl.ds(h * HEAD, HEAD)
        q = q_ref[:, cols]
        g = g_ref[:, cols]
        keys = jnp.concatenate([k_ref[:, cols]] + [r[0, :, cols] for r in fetched], axis=0)
        vals = jnp.concatenate([v_ref[:, cols]] + [r[1, :, cols] for r in fetched], axis=0)
        scores = lax.dot_general(q, keys, NT, preferred_element_type=jnp.float32) * scale
        highest = jnp.max(jnp.where(live, scores, -jnp.inf), axis=1, keepdims=True)
        total = jnp.sum(jnp.where(live, jnp.exp(scores - highest), 0.0), axis=1, keepdims=True)
        log_total = highest + jnp.log(total)
        prob = jnp.where(live, jnp.exp(scores - log_total), 0.0).astype(jnp.bfloat16)
        attended = jnp.dot(prob, vals, preferred_element_type=jnp.float32)
        delta = jnp.sum(g.astype(jnp.float32) * attended, axis=1, keepdims=True)
        prob_grad = lax.dot_general(g, vals, NT, preferred_element_type=jnp.float32)
        score_grad = (prob.astype(jnp.float32) * (prob_grad - delta) * scale).astype(jnp.bfloat16)
        dq_ref[:, cols] = jnp.dot(score_grad, keys, preferred_element_type=jnp.float32)
        grad_k = lax.dot_general(score_grad, q, TN, preferred_element_type=jnp.float32)
        grad_v = lax.dot_general(prob, g, TN, preferred_element_type=jnp.float32)
        dk_ref[:, cols] = grad_k[:rows]
        dv_ref[:, cols] = grad_v[:rows]
        for slot in range(slots):
            part = slice((slot + 1) * rows, (slot + 2) * rows)
            far[slot][0, :, cols] = grad_k[part].astype(jnp.bfloat16)
            far[slot][1, :, cols] = grad_v[part].astype(jnp.bfloat16)


def attention(live, q_norm, k_norm, value_rows, grad_rows, fetched):
    rows, features = q_norm.shape
    width = HEADS_PER_STEP * HEAD
    slots = len(fetched)
    tile = pl.BlockSpec((rows, width), lambda h: (0, h))
    pair = pl.BlockSpec((2, rows, width), lambda h: (0, 0, h))
    f32 = jax.ShapeDtypeStruct((rows, features), jnp.float32)
    bf16_pair = jax.ShapeDtypeStruct((2, rows, features), jnp.bfloat16)
    keys = rows * (slots + 1)
    flops = 2 * rows * keys * features * 6
    return pl.pallas_call(
        attention_kernel,
        grid=(features // width,),
        in_specs=[pl.BlockSpec(live.shape, lambda h: (0, 0))] + [tile] * 4 + [pair] * slots,
        out_specs=[tile] * 3 + [pair] * slots,
        out_shape=[f32] * 3 + [bf16_pair] * slots,
        cost_estimate=pl.CostEstimate(
            flops=flops,
            transcendentals=2 * rows * keys * (features // HEAD),
            bytes_accessed=2 * rows * features * (4 + 4 * slots) + 12 * rows * features,
        ),
    )(live, q_norm, k_norm, value_rows, grad_rows, *fetched)


def body(q_raw, k_raw, values, cotangent, q_gain, k_gain, key_tiles):
    tile_rows = q_raw.shape[1]
    features = q_raw.shape[2]
    offsets = level_offsets(LEVELS)
    q_hat, q_inv = normalize(q_raw[0])
    k_hat, k_inv = normalize(k_raw[0])
    q_norm = (q_hat * q_gain).astype(jnp.bfloat16)
    k_norm = (k_hat * k_gain).astype(jnp.bfloat16)
    value_rows = values[0]
    grad_rows = cotangent[0]
    entries = key_tiles[0]
    stacked = jnp.stack([k_norm, value_rows])
    fetched = fetch_neighbours(stacked, "seq")
    live = jnp.repeat(
        jnp.concatenate([jnp.ones((1,), jnp.int32), (entries >= 0).astype(jnp.int32)]), tile_rows
    )[None, :]
    q_norm_grad, k_norm_grad, v_sum, *far = attention(
        live, q_norm, k_norm, value_rows, grad_rows, fetched
    )
    for slot, offset in enumerate(offsets):
        back = from_behind(far[slot], "seq", offset)
        k_norm_grad = k_norm_grad + back[0].astype(jnp.float32)
        v_sum = v_sum + back[1].astype(jnp.float32)
    q_back, q_part = norm_backward(q_norm_grad, q_gain, q_hat, q_inv)
    k_back, k_part = norm_backward(k_norm_grad, k_gain, k_hat, k_inv)
    gain_grads = all_sum(jnp.concatenate([q_part, k_part]), ("dp", "seq"))
    q_gain_grad, k_gain_grad = gain_grads[:features], gain_grads[features:]
    return (
        q_back.astype(jnp.bfloat16)[None],
        k_back.astype(jnp.bfloat16)[None],
        v_sum.astype(jnp.bfloat16)[None],
        q_gain_grad,
        k_gain_grad,
    )


def solution(mesh):
    return jax.shard_map(
        body,
        mesh=mesh,
        in_specs=(
            P("dp", "seq", None),
            P("dp", "seq", None),
            P("dp", "seq", None),
            P("dp", "seq", None),
            P(),
            P(),
            P("seq", None),
        ),
        out_specs=(P("dp", "seq", None), P("dp", "seq", None), P("dp", "seq", None), P(), P()),
        check_vma=False,
    )
```

```python
import functools
import math

import jax
import jax.numpy as jnp
from jax import lax
from jax.experimental import pallas as pl
from jax.experimental.pallas import tpu as pltpu
from jax.sharding import PartitionSpec as P

HEAD = 128
LEVELS = 2
HEADS_PER_STEP = 4


EPS = 1e-06

NT = (((1,), (1,)), ((), ()))
TN = (((0,), (0,)), ((), ()))


def from_behind(value, axis, steps):
    count = lax.axis_size(axis)
    first, last = (max(0, -steps), min(count, count - steps))
    return lax.ppermute(value, axis, [(source, source + steps) for source in range(first, last)])


def pairs_permute(value, axis, pairs):
    count = lax.axis_size(axis)
    return lax.ppermute(value, axis, [(i, j) for i, j in pairs if 0 <= j < count])


def fetch_neighbours(value, axis):
    count = lax.axis_size(axis)
    behind = from_behind(value, axis, 1)
    ahead = from_behind(value, axis, -1)
    far_behind = pairs_permute(value, axis, [(i, i + 2) for i in range(0, count, 2)])
    far_ahead = pairs_permute(value, axis, [(i, i - 2) for i in range(1, count, 2)])
    relay_behind = pairs_permute(behind, axis, [(i, i + 1) for i in range(0, count, 2)])
    relay_ahead = pairs_permute(ahead, axis, [(i, i - 1) for i in range(1, count, 2)])
    odd = lax.axis_index(axis) % 2 == 1
    return [
        behind,
        ahead,
        jnp.where(odd, relay_behind, far_behind),
        jnp.where(odd, far_ahead, relay_ahead),
    ]


def return_parts(far, axis):
    count = lax.axis_size(axis)
    behind, ahead, far_behind, far_ahead = far
    odd = lax.axis_index(axis) % 2 == 1
    swapped = pairs_permute(
        jnp.where(odd, far_behind, far_ahead), axis, [(i, i ^ 1) for i in range(count)]
    )

    def joined(own):
        return (own.astype(jnp.float32) + swapped.astype(jnp.float32)).astype(jnp.bfloat16)

    to_next = from_behind(jnp.where(odd, joined(ahead), ahead), axis, 1)
    to_previous = from_behind(jnp.where(odd, behind, joined(behind)), axis, -1)
    two_ahead = pairs_permute(far_ahead, axis, [(i, i + 2) for i in range(1, count, 2)])
    two_behind = pairs_permute(far_behind, axis, [(i, i - 2) for i in range(0, count, 2)])
    return [to_next, to_previous, two_ahead, two_behind]


def all_sum(value, axes):
    for axis in axes:
        count = lax.axis_size(axis)
        bit = 1
        while bit < count:
            value = value + lax.ppermute(value, axis, [(i, i ^ bit) for i in range(count)])
            bit *= 2
    return value


def level_offsets(levels):
    return [sign * 2**level for level in range(levels) for sign in (-1, 1)]


def normalize(raw):
    numbers = raw.astype(jnp.float32)
    inverse = lax.rsqrt(jnp.mean(numbers * numbers, axis=-1, keepdims=True) + EPS)
    return (numbers * inverse, inverse)


def norm_backward(grad_norm, gain, hat, inverse):
    scaled = grad_norm * gain
    inner = jnp.mean(scaled * hat, axis=-1, keepdims=True)
    return (inverse * (scaled - hat * inner), jnp.sum(grad_norm * hat, axis=0))


def attention_kernel(live_ref, q_ref, k_ref, v_ref, g_ref, *refs):
    slots = (len(refs) - 3) // 2
    fetched = refs[:slots]
    dq_ref, dk_ref, dv_ref = refs[slots:slots + 3]
    far = refs[slots + 3:]
    rows = q_ref.shape[0]
    scale = 1.0 / math.sqrt(HEAD)
    live = live_ref[...] > 0
    for h in range(q_ref.shape[1] // HEAD):
        cols = pl.ds(h * HEAD, HEAD)
        q = q_ref[:, cols]
        g = g_ref[:, cols]
        keys = jnp.concatenate([k_ref[:, cols]] + [r[0, :, cols] for r in fetched], axis=0)
        vals = jnp.concatenate([v_ref[:, cols]] + [r[1, :, cols] for r in fetched], axis=0)
        scores = lax.dot_general(q, keys, NT, preferred_element_type=jnp.float32) * scale
        highest = jnp.max(jnp.where(live, scores, -jnp.inf), axis=1, keepdims=True)
        total = jnp.sum(jnp.where(live, jnp.exp(scores - highest), 0.0), axis=1, keepdims=True)
        log_total = highest + jnp.log(total)
        prob = jnp.where(live, jnp.exp(scores - log_total), 0.0).astype(jnp.bfloat16)
        attended = jnp.dot(prob, vals, preferred_element_type=jnp.float32)
        delta = jnp.sum(g.astype(jnp.float32) * attended, axis=1, keepdims=True)
        prob_grad = lax.dot_general(g, vals, NT, preferred_element_type=jnp.float32)
        score_grad = (prob.astype(jnp.float32) * (prob_grad - delta) * scale).astype(jnp.bfloat16)
        dq_ref[:, cols] = jnp.dot(score_grad, keys, preferred_element_type=jnp.float32)
        grad_k = lax.dot_general(score_grad, q, TN, preferred_element_type=jnp.float32)
        grad_v = lax.dot_general(prob, g, TN, preferred_element_type=jnp.float32)
        dk_ref[:, cols] = grad_k[:rows]
        dv_ref[:, cols] = grad_v[:rows]
        for slot in range(slots):
            part = slice((slot + 1) * rows, (slot + 2) * rows)
            far[slot][0, :, cols] = grad_k[part].astype(jnp.bfloat16)
            far[slot][1, :, cols] = grad_v[part].astype(jnp.bfloat16)


def attention(live, q_norm, k_norm, value_rows, grad_rows, fetched):
    rows, features = q_norm.shape
    width = HEADS_PER_STEP * HEAD
    slots = len(fetched)
    tile = pl.BlockSpec((rows, width), lambda h: (0, h))
    pair = pl.BlockSpec((2, rows, width), lambda h: (0, 0, h))
    f32 = jax.ShapeDtypeStruct((rows, features), jnp.float32)
    bf16_pair = jax.ShapeDtypeStruct((2, rows, features), jnp.bfloat16)
    keys = rows * (slots + 1)
    flops = 2 * rows * keys * features * 6
    return pl.pallas_call(
        attention_kernel,
        grid=(features // width,),
        in_specs=[pl.BlockSpec(live.shape, lambda h: (0, 0))] + [tile] * 4 + [pair] * slots,
        out_specs=[tile] * 3 + [pair] * slots,
        out_shape=[f32] * 3 + [bf16_pair] * slots,
        cost_estimate=pl.CostEstimate(
            flops=flops,
            transcendentals=2 * rows * keys * (features // HEAD),
            bytes_accessed=2 * rows * features * (4 + 4 * slots) + 12 * rows * features,
        ),
    )(live, q_norm, k_norm, value_rows, grad_rows, *fetched)


def body(q_raw, k_raw, values, cotangent, q_gain, k_gain, key_tiles):
    tile_rows = q_raw.shape[1]
    features = q_raw.shape[2]
    offsets = level_offsets(LEVELS)
    q_hat, q_inv = normalize(q_raw[0])
    k_hat, k_inv = normalize(k_raw[0])
    q_norm = (q_hat * q_gain).astype(jnp.bfloat16)
    k_norm = (k_hat * k_gain).astype(jnp.bfloat16)
    value_rows = values[0]
    grad_rows = cotangent[0]
    entries = key_tiles[0]
    stacked = jnp.stack([k_norm, value_rows])
    fetched = fetch_neighbours(stacked, "seq")
    live = jnp.repeat(
        jnp.concatenate([jnp.ones((1,), jnp.int32), (entries >= 0).astype(jnp.int32)]), tile_rows
    )[None, :]
    q_norm_grad, k_norm_grad, v_sum, *far = attention(
        live, q_norm, k_norm, value_rows, grad_rows, fetched
    )
    for back in return_parts(far, "seq"):
        k_norm_grad = k_norm_grad + back[0].astype(jnp.float32)
        v_sum = v_sum + back[1].astype(jnp.float32)
    q_back, q_part = norm_backward(q_norm_grad, q_gain, q_hat, q_inv)
    k_back, k_part = norm_backward(k_norm_grad, k_gain, k_hat, k_inv)
    gain_grads = all_sum(jnp.concatenate([q_part, k_part]), ("dp", "seq"))
    q_gain_grad, k_gain_grad = gain_grads[:features], gain_grads[features:]
    return (
        q_back.astype(jnp.bfloat16)[None],
        k_back.astype(jnp.bfloat16)[None],
        v_sum.astype(jnp.bfloat16)[None],
        q_gain_grad,
        k_gain_grad,
    )


def solution(mesh):
    return jax.shard_map(
        body,
        mesh=mesh,
        in_specs=(
            P("dp", "seq", None),
            P("dp", "seq", None),
            P("dp", "seq", None),
            P("dp", "seq", None),
            P(),
            P(),
            P("seq", None),
        ),
        out_specs=(P("dp", "seq", None), P("dp", "seq", None), P("dp", "seq", None), P(), P()),
        check_vma=False,
    )
```

```python
import functools
import math

import jax
import jax.numpy as jnp
from jax import lax
from jax.experimental import pallas as pl
from jax.experimental.pallas import tpu as pltpu
from jax.sharding import PartitionSpec as P

HEAD = 128
LEVELS = 2
HEADS_PER_STEP = 4


EPS = 1e-06

NT = (((1,), (1,)), ((), ()))
TN = (((0,), (0,)), ((), ()))


def from_behind(value, axis, steps):
    count = lax.axis_size(axis)
    first, last = (max(0, -steps), min(count, count - steps))
    return lax.ppermute(value, axis, [(source, source + steps) for source in range(first, last)])


def pairs_permute(value, axis, pairs):
    count = lax.axis_size(axis)
    return lax.ppermute(value, axis, [(i, j) for i, j in pairs if 0 <= j < count])


def fetch_neighbours(value, axis):
    count = lax.axis_size(axis)
    behind = from_behind(value, axis, 1)
    ahead = from_behind(value, axis, -1)
    far_behind = pairs_permute(value, axis, [(i, i + 2) for i in range(0, count, 2)])
    far_ahead = pairs_permute(value, axis, [(i, i - 2) for i in range(1, count, 2)])
    relay_behind = pairs_permute(behind, axis, [(i, i + 1) for i in range(0, count, 2)])
    relay_ahead = pairs_permute(ahead, axis, [(i, i - 1) for i in range(1, count, 2)])
    return [behind, ahead, far_behind, relay_behind, far_ahead, relay_ahead]


def return_parts(far, axis):
    count = lax.axis_size(axis)
    behind, ahead, far_behind, far_ahead = far
    odd = lax.axis_index(axis) % 2 == 1
    swapped = pairs_permute(
        jnp.where(odd, far_behind, far_ahead), axis, [(i, i ^ 1) for i in range(count)]
    )

    def joined(own):
        return (own.astype(jnp.float32) + swapped.astype(jnp.float32)).astype(jnp.bfloat16)

    to_next = from_behind(jnp.where(odd, joined(ahead), ahead), axis, 1)
    to_previous = from_behind(jnp.where(odd, behind, joined(behind)), axis, -1)
    two_ahead = pairs_permute(far_ahead, axis, [(i, i + 2) for i in range(1, count, 2)])
    two_behind = pairs_permute(far_behind, axis, [(i, i - 2) for i in range(0, count, 2)])
    return [to_next, to_previous, two_ahead, two_behind]


def all_sum(value, axes):
    for axis in axes:
        count = lax.axis_size(axis)
        bit = 1
        while bit < count:
            value = value + lax.ppermute(value, axis, [(i, i ^ bit) for i in range(count)])
            bit *= 2
    return value


def level_offsets(levels):
    return [sign * 2**level for level in range(levels) for sign in (-1, 1)]


def normalize(raw):
    numbers = raw.astype(jnp.float32)
    inverse = lax.rsqrt(jnp.mean(numbers * numbers, axis=-1, keepdims=True) + EPS)
    return (numbers * inverse, inverse)


def norm_backward(grad_norm, gain, hat, inverse):
    scaled = grad_norm * gain
    inner = jnp.mean(scaled * hat, axis=-1, keepdims=True)
    return (inverse * (scaled - hat * inner), jnp.sum(grad_norm * hat, axis=0))


def attention_kernel(odd_ref, bias_ref, q_ref, k_ref, v_ref, g_ref, *refs):
    behind, ahead, far_behind, relay_behind, far_ahead, relay_ahead = refs[:6]
    dq_ref, dk_ref, dv_ref = refs[6:9]
    far = refs[9:]
    slots = len(far)
    rows = q_ref.shape[0]
    scale = 1.0 / math.sqrt(HEAD)
    odd = odd_ref[0] == 1
    bias = bias_ref[...]
    for h in range(q_ref.shape[1] // HEAD):
        cols = pl.ds(h * HEAD, HEAD)

        def pick(which, cols=cols):
            return jnp.concatenate(
                [
                    behind[which, :, cols],
                    ahead[which, :, cols],
                    jnp.where(odd, relay_behind[which, :, cols], far_behind[which, :, cols]),
                    jnp.where(odd, far_ahead[which, :, cols], relay_ahead[which, :, cols]),
                ],
                axis=0,
            )

        q = q_ref[:, cols]
        g = g_ref[:, cols]
        keys = jnp.concatenate([k_ref[:, cols], pick(0)], axis=0)
        vals = jnp.concatenate([v_ref[:, cols], pick(1)], axis=0)
        scores = lax.dot_general(q, keys, NT, preferred_element_type=jnp.float32) * scale + bias
        highest = jnp.max(scores, axis=1, keepdims=True)
        total = jnp.sum(jnp.exp(scores - highest), axis=1, keepdims=True)
        log_total = highest + jnp.log(total)
        prob = jnp.exp(scores - log_total).astype(jnp.bfloat16)
        attended = jnp.dot(prob, vals, preferred_element_type=jnp.float32)
        delta = jnp.sum(g.astype(jnp.float32) * attended, axis=1, keepdims=True)
        prob_grad = lax.dot_general(g, vals, NT, preferred_element_type=jnp.float32)
        score_grad = (prob.astype(jnp.float32) * (prob_grad - delta) * scale).astype(jnp.bfloat16)
        dq_ref[:, cols] = jnp.dot(score_grad, keys, preferred_element_type=jnp.float32)
        grad_k = lax.dot_general(score_grad, q, TN, preferred_element_type=jnp.float32)
        grad_v = lax.dot_general(prob, g, TN, preferred_element_type=jnp.float32)
        dk_ref[:, cols] = grad_k[:rows]
        dv_ref[:, cols] = grad_v[:rows]
        for slot in range(slots):
            part = slice((slot + 1) * rows, (slot + 2) * rows)
            far[slot][0, :, cols] = grad_k[part].astype(jnp.bfloat16)
            far[slot][1, :, cols] = grad_v[part].astype(jnp.bfloat16)


def attention(odd, bias, q_norm, k_norm, value_rows, grad_rows, fetched):
    rows, features = q_norm.shape
    width = HEADS_PER_STEP * HEAD
    slots = 4
    tile = pl.BlockSpec((rows, width), lambda h, odd: (0, h))
    pair = pl.BlockSpec((2, rows, width), lambda h, odd: (0, 0, h))
    f32 = jax.ShapeDtypeStruct((rows, features), jnp.float32)
    bf16_pair = jax.ShapeDtypeStruct((2, rows, features), jnp.bfloat16)
    keys = rows * (slots + 1)
    flops = 2 * rows * keys * features * 6
    grid_spec = pltpu.PrefetchScalarGridSpec(
        num_scalar_prefetch=1,
        grid=(features // width,),
        in_specs=[pl.BlockSpec(bias.shape, lambda h, odd: (0, 0))] + [tile] * 4 + [pair] * len(fetched),
        out_specs=[tile] * 3 + [pair] * slots,
    )
    return pl.pallas_call(
        attention_kernel,
        grid_spec=grid_spec,
        out_shape=[f32] * 3 + [bf16_pair] * slots,
        cost_estimate=pl.CostEstimate(
            flops=flops,
            transcendentals=2 * rows * keys * (features // HEAD),
            bytes_accessed=2 * rows * features * (4 + 2 * len(fetched)) + 12 * rows * features,
        ),
    )(odd, bias, q_norm, k_norm, value_rows, grad_rows, *fetched)


def body(q_raw, k_raw, values, cotangent, q_gain, k_gain, key_tiles):
    tile_rows = q_raw.shape[1]
    features = q_raw.shape[2]
    offsets = level_offsets(LEVELS)
    q_hat, q_inv = normalize(q_raw[0])
    k_hat, k_inv = normalize(k_raw[0])
    q_norm = (q_hat * q_gain).astype(jnp.bfloat16)
    k_norm = (k_hat * k_gain).astype(jnp.bfloat16)
    value_rows = values[0]
    grad_rows = cotangent[0]
    entries = key_tiles[0]
    stacked = jnp.stack([k_norm, value_rows])
    fetched = fetch_neighbours(stacked, "seq")
    live = jnp.concatenate([jnp.ones((1,), bool), entries >= 0])
    bias = jnp.repeat(jnp.where(live, 0.0, -jnp.inf).astype(jnp.float32), tile_rows)[None, :]
    odd = (lax.axis_index("seq") % 2).astype(jnp.int32)[None]
    q_norm_grad, k_norm_grad, v_sum, *far = attention(
        odd, bias, q_norm, k_norm, value_rows, grad_rows, fetched
    )
    for back in return_parts(far, "seq"):
        k_norm_grad = k_norm_grad + back[0].astype(jnp.float32)
        v_sum = v_sum + back[1].astype(jnp.float32)
    q_back, q_part = norm_backward(q_norm_grad, q_gain, q_hat, q_inv)
    k_back, k_part = norm_backward(k_norm_grad, k_gain, k_hat, k_inv)
    gain_grads = all_sum(jnp.concatenate([q_part, k_part]), ("dp", "seq"))
    q_gain_grad, k_gain_grad = gain_grads[:features], gain_grads[features:]
    return (
        q_back.astype(jnp.bfloat16)[None],
        k_back.astype(jnp.bfloat16)[None],
        v_sum.astype(jnp.bfloat16)[None],
        q_gain_grad,
        k_gain_grad,
    )


def solution(mesh):
    return jax.shard_map(
        body,
        mesh=mesh,
        in_specs=(
            P("dp", "seq", None),
            P("dp", "seq", None),
            P("dp", "seq", None),
            P("dp", "seq", None),
            P(),
            P(),
            P("seq", None),
        ),
        out_specs=(P("dp", "seq", None), P("dp", "seq", None), P("dp", "seq", None), P(), P()),
        check_vma=False,
    )
```

```python
import functools
import math

import jax
import jax.numpy as jnp
from jax import lax
from jax.experimental import pallas as pl
from jax.experimental.pallas import tpu as pltpu
from jax.sharding import PartitionSpec as P

HEAD = 128
LEVELS = 2
HEADS_PER_STEP = 2
CHUNKS = 2


EPS = 1e-06

NT = (((1,), (1,)), ((), ()))
TN = (((0,), (0,)), ((), ()))


def from_behind(value, axis, steps):
    count = lax.axis_size(axis)
    first, last = (max(0, -steps), min(count, count - steps))
    return lax.ppermute(value, axis, [(source, source + steps) for source in range(first, last)])


def pairs_permute(value, axis, pairs):
    count = lax.axis_size(axis)
    return lax.ppermute(value, axis, [(i, j) for i, j in pairs if 0 <= j < count])


def fetch_neighbours(value, axis):
    count = lax.axis_size(axis)
    behind = from_behind(value, axis, 1)
    ahead = from_behind(value, axis, -1)
    far_behind = pairs_permute(value, axis, [(i, i + 2) for i in range(0, count, 2)])
    far_ahead = pairs_permute(value, axis, [(i, i - 2) for i in range(1, count, 2)])
    relay_behind = pairs_permute(behind, axis, [(i, i + 1) for i in range(0, count, 2)])
    relay_ahead = pairs_permute(ahead, axis, [(i, i - 1) for i in range(1, count, 2)])
    return [behind, ahead, far_behind, relay_behind, far_ahead, relay_ahead]


def return_parts(far, axis):
    count = lax.axis_size(axis)
    behind, ahead, far_behind, far_ahead = far
    odd = lax.axis_index(axis) % 2 == 1
    swapped = pairs_permute(
        jnp.where(odd, far_behind, far_ahead), axis, [(i, i ^ 1) for i in range(count)]
    )

    def joined(own):
        return (own.astype(jnp.float32) + swapped.astype(jnp.float32)).astype(jnp.bfloat16)

    to_next = from_behind(jnp.where(odd, joined(ahead), ahead), axis, 1)
    to_previous = from_behind(jnp.where(odd, behind, joined(behind)), axis, -1)
    two_ahead = pairs_permute(far_ahead, axis, [(i, i + 2) for i in range(1, count, 2)])
    two_behind = pairs_permute(far_behind, axis, [(i, i - 2) for i in range(0, count, 2)])
    return [to_next, to_previous, two_ahead, two_behind]


def all_sum(value, axes):
    for axis in axes:
        count = lax.axis_size(axis)
        bit = 1
        while bit < count:
            value = value + lax.ppermute(value, axis, [(i, i ^ bit) for i in range(count)])
            bit *= 2
    return value


def level_offsets(levels):
    return [sign * 2**level for level in range(levels) for sign in (-1, 1)]


def normalize(raw):
    numbers = raw.astype(jnp.float32)
    inverse = lax.rsqrt(jnp.mean(numbers * numbers, axis=-1, keepdims=True) + EPS)
    return (numbers * inverse, inverse)


def norm_backward(grad_norm, gain, hat, inverse):
    scaled = grad_norm * gain
    inner = jnp.mean(scaled * hat, axis=-1, keepdims=True)
    return (inverse * (scaled - hat * inner), jnp.sum(grad_norm * hat, axis=0))


def attention_kernel(odd_ref, bias_ref, q_ref, k_ref, v_ref, g_ref, *refs):
    behind, ahead, far_behind, relay_behind, far_ahead, relay_ahead = refs[:6]
    dq_ref, dk_ref, dv_ref = refs[6:9]
    far = refs[9:]
    slots = len(far)
    rows = q_ref.shape[0]
    scale = 1.0 / math.sqrt(HEAD)
    odd = odd_ref[0] == 1
    bias = bias_ref[...]
    for h in range(q_ref.shape[1] // HEAD):
        cols = pl.ds(h * HEAD, HEAD)

        def pick(which, cols=cols):
            return jnp.concatenate(
                [
                    behind[which, :, cols],
                    ahead[which, :, cols],
                    jnp.where(odd, relay_behind[which, :, cols], far_behind[which, :, cols]),
                    jnp.where(odd, far_ahead[which, :, cols], relay_ahead[which, :, cols]),
                ],
                axis=0,
            )

        q = q_ref[:, cols]
        g = g_ref[:, cols]
        keys = jnp.concatenate([k_ref[:, cols], pick(0)], axis=0)
        vals = jnp.concatenate([v_ref[:, cols], pick(1)], axis=0)
        scores = lax.dot_general(q, keys, NT, preferred_element_type=jnp.float32) * scale + bias
        highest = jnp.max(scores, axis=1, keepdims=True)
        total = jnp.sum(jnp.exp(scores - highest), axis=1, keepdims=True)
        log_total = highest + jnp.log(total)
        prob = jnp.exp(scores - log_total).astype(jnp.bfloat16)
        attended = jnp.dot(prob, vals, preferred_element_type=jnp.float32)
        delta = jnp.sum(g.astype(jnp.float32) * attended, axis=1, keepdims=True)
        prob_grad = lax.dot_general(g, vals, NT, preferred_element_type=jnp.float32)
        score_grad = (prob.astype(jnp.float32) * (prob_grad - delta) * scale).astype(jnp.bfloat16)
        dq_ref[:, cols] = jnp.dot(score_grad, keys, preferred_element_type=jnp.float32)
        grad_k = lax.dot_general(score_grad, q, TN, preferred_element_type=jnp.float32)
        grad_v = lax.dot_general(prob, g, TN, preferred_element_type=jnp.float32)
        dk_ref[:, cols] = grad_k[:rows]
        dv_ref[:, cols] = grad_v[:rows]
        for slot in range(slots):
            part = slice((slot + 1) * rows, (slot + 2) * rows)
            far[slot][0, :, cols] = grad_k[part].astype(jnp.bfloat16)
            far[slot][1, :, cols] = grad_v[part].astype(jnp.bfloat16)


def attention(odd, bias, q_norm, k_norm, value_rows, grad_rows, fetched, first=0):
    rows = q_norm.shape[0]
    features = fetched[0].shape[2]
    width = HEADS_PER_STEP * HEAD
    slots = 4
    own = pl.BlockSpec((rows, width), lambda h, odd: (0, h + first))
    tile = pl.BlockSpec((rows, width), lambda h, odd: (0, h))
    pair = pl.BlockSpec((2, rows, width), lambda h, odd: (0, 0, h))
    f32 = jax.ShapeDtypeStruct((rows, features), jnp.float32)
    bf16_pair = jax.ShapeDtypeStruct((2, rows, features), jnp.bfloat16)
    keys = rows * (slots + 1)
    flops = 2 * rows * keys * features * 6
    grid_spec = pltpu.PrefetchScalarGridSpec(
        num_scalar_prefetch=1,
        grid=(features // width,),
        in_specs=[pl.BlockSpec(bias.shape, lambda h, odd: (0, 0))] + [own] * 4 + [pair] * len(fetched),
        out_specs=[tile] * 3 + [pair] * slots,
    )
    return pl.pallas_call(
        attention_kernel,
        grid_spec=grid_spec,
        out_shape=[f32] * 3 + [bf16_pair] * slots,
        cost_estimate=pl.CostEstimate(
            flops=flops,
            transcendentals=2 * rows * keys * (features // HEAD),
            bytes_accessed=2 * rows * features * (4 + 2 * len(fetched)) + 12 * rows * features,
        ),
    )(odd, bias, q_norm, k_norm, value_rows, grad_rows, *fetched)


def body(q_raw, k_raw, values, cotangent, q_gain, k_gain, key_tiles):
    tile_rows = q_raw.shape[1]
    features = q_raw.shape[2]
    offsets = level_offsets(LEVELS)
    q_hat, q_inv = normalize(q_raw[0])
    k_hat, k_inv = normalize(k_raw[0])
    q_norm = (q_hat * q_gain).astype(jnp.bfloat16)
    k_norm = (k_hat * k_gain).astype(jnp.bfloat16)
    value_rows = values[0]
    grad_rows = cotangent[0]
    entries = key_tiles[0]
    live = jnp.concatenate([jnp.ones((1,), bool), entries >= 0])
    bias = jnp.repeat(jnp.where(live, 0.0, -jnp.inf).astype(jnp.float32), tile_rows)[None, :]
    odd = (lax.axis_index("seq") % 2).astype(jnp.int32)[None]
    chunk = features // CHUNKS
    pieces = []
    fetched = None
    for c in range(CHUNKS):
        cols = slice(c * chunk, (c + 1) * chunk)
        stacked = jnp.stack([k_norm[:, cols], value_rows[:, cols]])
        if fetched is not None:
            stacked, _ = lax.optimization_barrier((stacked, fetched))
        fetched = fetch_neighbours(stacked, "seq")
        q_grad_c, k_grad_c, v_sum_c, *far = attention(
            odd, bias, q_norm, k_norm, value_rows, grad_rows, fetched, c * chunk // (HEADS_PER_STEP * HEAD)
        )
        for back in return_parts(far, "seq"):
            k_grad_c = k_grad_c + back[0].astype(jnp.float32)
            v_sum_c = v_sum_c + back[1].astype(jnp.float32)
        pieces.append((q_grad_c, k_grad_c, v_sum_c))
    q_norm_grad, k_norm_grad, v_sum = (
        jnp.concatenate([p[i] for p in pieces], axis=1) for i in range(3)
    )
    q_back, q_part = norm_backward(q_norm_grad, q_gain, q_hat, q_inv)
    k_back, k_part = norm_backward(k_norm_grad, k_gain, k_hat, k_inv)
    gain_grads = all_sum(jnp.concatenate([q_part, k_part]), ("dp", "seq"))
    q_gain_grad, k_gain_grad = gain_grads[:features], gain_grads[features:]
    return (
        q_back.astype(jnp.bfloat16)[None],
        k_back.astype(jnp.bfloat16)[None],
        v_sum.astype(jnp.bfloat16)[None],
        q_gain_grad,
        k_gain_grad,
    )


def solution(mesh):
    return jax.shard_map(
        body,
        mesh=mesh,
        in_specs=(
            P("dp", "seq", None),
            P("dp", "seq", None),
            P("dp", "seq", None),
            P("dp", "seq", None),
            P(),
            P(),
            P("seq", None),
        ),
        out_specs=(P("dp", "seq", None), P("dp", "seq", None), P("dp", "seq", None), P(), P()),
        check_vma=False,
    )
```

```python
import functools
import math

import jax
import jax.numpy as jnp
from jax import lax
from jax.experimental import pallas as pl
from jax.experimental.pallas import tpu as pltpu
from jax.sharding import PartitionSpec as P

HEAD = 128
LEVELS = 2
HEADS_PER_STEP = 5
CHUNKS = 4


EPS = 1e-06

NT = (((1,), (1,)), ((), ()))
TN = (((0,), (0,)), ((), ()))


def from_behind(value, axis, steps):
    count = lax.axis_size(axis)
    first, last = (max(0, -steps), min(count, count - steps))
    return lax.ppermute(value, axis, [(source, source + steps) for source in range(first, last)])


def pairs_permute(value, axis, pairs):
    count = lax.axis_size(axis)
    return lax.ppermute(value, axis, [(i, j) for i, j in pairs if 0 <= j < count])


def fetch_neighbours(value, axis):
    count = lax.axis_size(axis)
    behind = from_behind(value, axis, 1)
    ahead = from_behind(value, axis, -1)
    far_behind = pairs_permute(value, axis, [(i, i + 2) for i in range(0, count, 2)])
    far_ahead = pairs_permute(value, axis, [(i, i - 2) for i in range(1, count, 2)])
    relay_behind = pairs_permute(behind, axis, [(i, i + 1) for i in range(0, count, 2)])
    relay_ahead = pairs_permute(ahead, axis, [(i, i - 1) for i in range(1, count, 2)])
    return [behind, ahead, far_behind, relay_behind, far_ahead, relay_ahead]


def return_parts(far, axis):
    count = lax.axis_size(axis)
    behind, ahead, far_behind, far_ahead = far
    odd = lax.axis_index(axis) % 2 == 1
    swapped = pairs_permute(
        jnp.where(odd, far_behind, far_ahead), axis, [(i, i ^ 1) for i in range(count)]
    )

    def joined(own):
        return (own.astype(jnp.float32) + swapped.astype(jnp.float32)).astype(jnp.bfloat16)

    to_next = from_behind(jnp.where(odd, joined(ahead), ahead), axis, 1)
    to_previous = from_behind(jnp.where(odd, behind, joined(behind)), axis, -1)
    two_ahead = pairs_permute(far_ahead, axis, [(i, i + 2) for i in range(1, count, 2)])
    two_behind = pairs_permute(far_behind, axis, [(i, i - 2) for i in range(0, count, 2)])
    return [to_next, to_previous, two_ahead, two_behind]


def all_sum(value, axes):
    for axis in axes:
        count = lax.axis_size(axis)
        bit = 1
        while bit < count:
            value = value + lax.ppermute(value, axis, [(i, i ^ bit) for i in range(count)])
            bit *= 2
    return value


def level_offsets(levels):
    return [sign * 2**level for level in range(levels) for sign in (-1, 1)]


def normalize(raw):
    numbers = raw.astype(jnp.float32)
    inverse = lax.rsqrt(jnp.mean(numbers * numbers, axis=-1, keepdims=True) + EPS)
    return (numbers * inverse, inverse)


def norm_backward(grad_norm, gain, hat, inverse):
    scaled = grad_norm * gain
    inner = jnp.mean(scaled * hat, axis=-1, keepdims=True)
    return (inverse * (scaled - hat * inner), jnp.sum(grad_norm * hat, axis=0))


def attention_kernel(odd_ref, bias_ref, q_ref, k_ref, v_ref, g_ref, *refs):
    behind, ahead, far_behind, relay_behind, far_ahead, relay_ahead = refs[:6]
    dq_ref, dk_ref, dv_ref = refs[6:9]
    far = refs[9:]
    slots = len(far)
    rows = q_ref.shape[0]
    scale = 1.0 / math.sqrt(HEAD)
    odd = odd_ref[0] == 1
    bias = bias_ref[...]
    for h in range(q_ref.shape[1] // HEAD):
        cols = pl.ds(h * HEAD, HEAD)

        def pick(which, cols=cols):
            return jnp.concatenate(
                [
                    behind[which, :, cols],
                    ahead[which, :, cols],
                    jnp.where(odd, relay_behind[which, :, cols], far_behind[which, :, cols]),
                    jnp.where(odd, far_ahead[which, :, cols], relay_ahead[which, :, cols]),
                ],
                axis=0,
            )

        q = q_ref[:, cols]
        g = g_ref[:, cols]
        keys = jnp.concatenate([k_ref[:, cols], pick(0)], axis=0)
        vals = jnp.concatenate([v_ref[:, cols], pick(1)], axis=0)
        scores = lax.dot_general(q, keys, NT, preferred_element_type=jnp.float32) * scale + bias
        highest = jnp.max(scores, axis=1, keepdims=True)
        total = jnp.sum(jnp.exp(scores - highest), axis=1, keepdims=True)
        log_total = highest + jnp.log(total)
        prob = jnp.exp(scores - log_total).astype(jnp.bfloat16)
        attended = jnp.dot(prob, vals, preferred_element_type=jnp.float32)
        delta = jnp.sum(g.astype(jnp.float32) * attended, axis=1, keepdims=True)
        prob_grad = lax.dot_general(g, vals, NT, preferred_element_type=jnp.float32)
        score_grad = (prob.astype(jnp.float32) * (prob_grad - delta) * scale).astype(jnp.bfloat16)
        dq_ref[:, cols] = jnp.dot(score_grad, keys, preferred_element_type=jnp.float32)
        grad_k = lax.dot_general(score_grad, q, TN, preferred_element_type=jnp.float32)
        grad_v = lax.dot_general(prob, g, TN, preferred_element_type=jnp.float32)
        dk_ref[:, cols] = grad_k[:rows]
        dv_ref[:, cols] = grad_v[:rows]
        for slot in range(slots):
            part = slice((slot + 1) * rows, (slot + 2) * rows)
            far[slot][0, :, cols] = grad_k[part].astype(jnp.bfloat16)
            far[slot][1, :, cols] = grad_v[part].astype(jnp.bfloat16)


def attention(odd, bias, q_norm, k_norm, value_rows, grad_rows, fetched, first=0):
    rows = q_norm.shape[0]
    features = fetched[0].shape[2]
    width = HEADS_PER_STEP * HEAD
    slots = 4
    own = pl.BlockSpec((rows, width), lambda h, odd: (0, h + first))
    tile = pl.BlockSpec((rows, width), lambda h, odd: (0, h))
    pair = pl.BlockSpec((2, rows, width), lambda h, odd: (0, 0, h))
    f32 = jax.ShapeDtypeStruct((rows, features), jnp.float32)
    bf16_pair = jax.ShapeDtypeStruct((2, rows, features), jnp.bfloat16)
    keys = rows * (slots + 1)
    flops = 2 * rows * keys * features * 6
    grid_spec = pltpu.PrefetchScalarGridSpec(
        num_scalar_prefetch=1,
        grid=(features // width,),
        in_specs=[pl.BlockSpec(bias.shape, lambda h, odd: (0, 0))] + [own] * 4 + [pair] * len(fetched),
        out_specs=[tile] * 3 + [pair] * slots,
    )
    return pl.pallas_call(
        attention_kernel,
        grid_spec=grid_spec,
        out_shape=[f32] * 3 + [bf16_pair] * slots,
        cost_estimate=pl.CostEstimate(
            flops=flops,
            transcendentals=2 * rows * keys * (features // HEAD),
            bytes_accessed=2 * rows * features * (4 + 2 * len(fetched)) + 12 * rows * features,
        ),
    )(odd, bias, q_norm, k_norm, value_rows, grad_rows, *fetched)


def body(q_raw, k_raw, values, cotangent, q_gain, k_gain, key_tiles):
    tile_rows = q_raw.shape[1]
    features = q_raw.shape[2]
    offsets = level_offsets(LEVELS)
    q_hat, q_inv = normalize(q_raw[0])
    k_hat, k_inv = normalize(k_raw[0])
    q_norm = (q_hat * q_gain).astype(jnp.bfloat16)
    k_norm = (k_hat * k_gain).astype(jnp.bfloat16)
    value_rows = values[0]
    grad_rows = cotangent[0]
    entries = key_tiles[0]
    live = jnp.concatenate([jnp.ones((1,), bool), entries >= 0])
    bias = jnp.repeat(jnp.where(live, 0.0, -jnp.inf).astype(jnp.float32), tile_rows)[None, :]
    odd = (lax.axis_index("seq") % 2).astype(jnp.int32)[None]
    chunk = features // CHUNKS
    pieces = []
    fetched = None
    for c in range(CHUNKS):
        cols = slice(c * chunk, (c + 1) * chunk)
        stacked = jnp.stack([k_norm[:, cols], value_rows[:, cols]])
        if fetched is not None:
            stacked, _ = lax.optimization_barrier((stacked, fetched))
        fetched = fetch_neighbours(stacked, "seq")
        q_grad_c, k_grad_c, v_sum_c, *far = attention(
            odd, bias, q_norm, k_norm, value_rows, grad_rows, fetched, c * chunk // (HEADS_PER_STEP * HEAD)
        )
        for back in return_parts(far, "seq"):
            k_grad_c = k_grad_c + back[0].astype(jnp.float32)
            v_sum_c = v_sum_c + back[1].astype(jnp.float32)
        pieces.append((q_grad_c, k_grad_c, v_sum_c))
    q_norm_grad, k_norm_grad, v_sum = (
        jnp.concatenate([p[i] for p in pieces], axis=1) for i in range(3)
    )
    q_back, q_part = norm_backward(q_norm_grad, q_gain, q_hat, q_inv)
    k_back, k_part = norm_backward(k_norm_grad, k_gain, k_hat, k_inv)
    gain_grads = all_sum(jnp.concatenate([q_part, k_part]), ("dp", "seq"))
    q_gain_grad, k_gain_grad = gain_grads[:features], gain_grads[features:]
    return (
        q_back.astype(jnp.bfloat16)[None],
        k_back.astype(jnp.bfloat16)[None],
        v_sum.astype(jnp.bfloat16)[None],
        q_gain_grad,
        k_gain_grad,
    )


def solution(mesh):
    return jax.shard_map(
        body,
        mesh=mesh,
        in_specs=(
            P("dp", "seq", None),
            P("dp", "seq", None),
            P("dp", "seq", None),
            P("dp", "seq", None),
            P(),
            P(),
            P("seq", None),
        ),
        out_specs=(P("dp", "seq", None), P("dp", "seq", None), P("dp", "seq", None), P(), P()),
        check_vma=False,
    )
```

```python
import functools
import math

import jax
import jax.numpy as jnp
from jax import lax
from jax.experimental import pallas as pl
from jax.experimental.pallas import tpu as pltpu
from jax.sharding import PartitionSpec as P

HEAD = 128
LEVELS = 2
HEADS_PER_STEP = 2
CHUNKS = 2


EPS = 1e-06

NT = (((1,), (1,)), ((), ()))
TN = (((0,), (0,)), ((), ()))


def from_behind(value, axis, steps):
    count = lax.axis_size(axis)
    first, last = (max(0, -steps), min(count, count - steps))
    return lax.ppermute(value, axis, [(source, source + steps) for source in range(first, last)])


def pairs_permute(value, axis, pairs):
    count = lax.axis_size(axis)
    return lax.ppermute(value, axis, [(i, j) for i, j in pairs if 0 <= j < count])


def fetch_neighbours(value, axis):
    count = lax.axis_size(axis)
    behind = from_behind(value, axis, 1)
    ahead = from_behind(value, axis, -1)
    two = [(i, i + 2) for i in range(0, count, 2)] + [(i, i - 2) for i in range(1, count, 2)]
    far2 = pairs_permute(value, axis, two)
    odd = lax.axis_index(axis) % 2 == 1
    relay = pairs_permute(jnp.where(odd, ahead, behind), axis, [(i, i ^ 1) for i in range(count)])
    return [behind, ahead, far2, relay]


def return_parts(far, axis):
    count = lax.axis_size(axis)
    behind, ahead, for_partner, direct = far
    odd = lax.axis_index(axis) % 2 == 1
    swapped = pairs_permute(for_partner, axis, [(i, i ^ 1) for i in range(count)])

    def joined(own):
        return (own.astype(jnp.float32) + swapped.astype(jnp.float32)).astype(jnp.bfloat16)

    to_next = from_behind(jnp.where(odd, joined(ahead), ahead), axis, 1)
    to_previous = from_behind(jnp.where(odd, behind, joined(behind)), axis, -1)
    two = [(i, i + 2) for i in range(1, count, 2)] + [(i, i - 2) for i in range(0, count, 2)]
    return [to_next, to_previous, pairs_permute(direct, axis, two)]


def all_sum(value, axes):
    for axis in axes:
        count = lax.axis_size(axis)
        bit = 1
        while bit < count:
            value = value + lax.ppermute(value, axis, [(i, i ^ bit) for i in range(count)])
            bit *= 2
    return value


def level_offsets(levels):
    return [sign * 2**level for level in range(levels) for sign in (-1, 1)]


def normalize(raw):
    numbers = raw.astype(jnp.float32)
    inverse = lax.rsqrt(jnp.mean(numbers * numbers, axis=-1, keepdims=True) + EPS)
    return (numbers * inverse, inverse)


def norm_backward(grad_norm, gain, hat, inverse):
    scaled = grad_norm * gain
    inner = jnp.mean(scaled * hat, axis=-1, keepdims=True)
    return (inverse * (scaled - hat * inner), jnp.sum(grad_norm * hat, axis=0))


def attention_kernel(odd_ref, bias_ref, q_ref, k_ref, v_ref, g_ref, *refs):
    behind, ahead, far2, relay = refs[:4]
    dq_ref, dk_ref, dv_ref = refs[4:7]
    far = refs[7:]
    slots = len(far)
    rows = q_ref.shape[0]
    scale = 1.0 / math.sqrt(HEAD)
    odd = odd_ref[0] == 1
    bias = bias_ref[...]
    for h in range(q_ref.shape[1] // HEAD):
        cols = pl.ds(h * HEAD, HEAD)

        def pick(which, cols=cols):
            return jnp.concatenate(
                [
                    behind[which, :, cols],
                    ahead[which, :, cols],
                    jnp.where(odd, relay[which, :, cols], far2[which, :, cols]),
                    jnp.where(odd, far2[which, :, cols], relay[which, :, cols]),
                ],
                axis=0,
            )

        q = q_ref[:, cols]
        g = g_ref[:, cols]
        keys = jnp.concatenate([k_ref[:, cols], pick(0)], axis=0)
        vals = jnp.concatenate([v_ref[:, cols], pick(1)], axis=0)
        scores = lax.dot_general(q, keys, NT, preferred_element_type=jnp.float32) * scale + bias
        highest = jnp.max(scores, axis=1, keepdims=True)
        total = jnp.sum(jnp.exp(scores - highest), axis=1, keepdims=True)
        log_total = highest + jnp.log(total)
        prob = jnp.exp(scores - log_total).astype(jnp.bfloat16)
        attended = jnp.dot(prob, vals, preferred_element_type=jnp.float32)
        delta = jnp.sum(g.astype(jnp.float32) * attended, axis=1, keepdims=True)
        prob_grad = lax.dot_general(g, vals, NT, preferred_element_type=jnp.float32)
        score_grad = (prob.astype(jnp.float32) * (prob_grad - delta) * scale).astype(jnp.bfloat16)
        dq_ref[:, cols] = jnp.dot(score_grad, keys, preferred_element_type=jnp.float32)
        grad_k = lax.dot_general(score_grad, q, TN, preferred_element_type=jnp.float32)
        grad_v = lax.dot_general(prob, g, TN, preferred_element_type=jnp.float32)
        dk_ref[:, cols] = grad_k[:rows]
        dv_ref[:, cols] = grad_v[:rows]
        parts = [
            (grad_k[(slot + 1) * rows:(slot + 2) * rows].astype(jnp.bfloat16),
             grad_v[(slot + 1) * rows:(slot + 2) * rows].astype(jnp.bfloat16))
            for slot in range(slots)
        ]
        arranged = [
            parts[0],
            parts[1],
            tuple(jnp.where(odd, a, b) for a, b in zip(parts[2], parts[3])),
            tuple(jnp.where(odd, b, a) for a, b in zip(parts[2], parts[3])),
        ]
        for slot, (part_k, part_v) in enumerate(arranged):
            far[slot][0, :, cols] = part_k
            far[slot][1, :, cols] = part_v


def attention(odd, bias, q_norm, k_norm, value_rows, grad_rows, fetched, first=0):
    rows = q_norm.shape[0]
    features = fetched[0].shape[2]
    width = HEADS_PER_STEP * HEAD
    slots = 4
    own = pl.BlockSpec((rows, width), lambda h, odd: (0, h + first))
    tile = pl.BlockSpec((rows, width), lambda h, odd: (0, h))
    pair = pl.BlockSpec((2, rows, width), lambda h, odd: (0, 0, h))
    f32 = jax.ShapeDtypeStruct((rows, features), jnp.float32)
    bf16_pair = jax.ShapeDtypeStruct((2, rows, features), jnp.bfloat16)
    keys = rows * (slots + 1)
    flops = 2 * rows * keys * features * 6
    grid_spec = pltpu.PrefetchScalarGridSpec(
        num_scalar_prefetch=1,
        grid=(features // width,),
        in_specs=[pl.BlockSpec(bias.shape, lambda h, odd: (0, 0))] + [own] * 4 + [pair] * len(fetched),
        out_specs=[tile] * 3 + [pair] * slots,
    )
    return pl.pallas_call(
        attention_kernel,
        grid_spec=grid_spec,
        out_shape=[f32] * 3 + [bf16_pair] * slots,
        cost_estimate=pl.CostEstimate(
            flops=flops,
            transcendentals=2 * rows * keys * (features // HEAD),
            bytes_accessed=2 * rows * features * (4 + 2 * len(fetched)) + 12 * rows * features,
        ),
    )(odd, bias, q_norm, k_norm, value_rows, grad_rows, *fetched)


def body(q_raw, k_raw, values, cotangent, q_gain, k_gain, key_tiles):
    tile_rows = q_raw.shape[1]
    features = q_raw.shape[2]
    offsets = level_offsets(LEVELS)
    q_hat, q_inv = normalize(q_raw[0])
    k_hat, k_inv = normalize(k_raw[0])
    q_norm = (q_hat * q_gain).astype(jnp.bfloat16)
    k_norm = (k_hat * k_gain).astype(jnp.bfloat16)
    value_rows = values[0]
    grad_rows = cotangent[0]
    entries = key_tiles[0]
    live = jnp.concatenate([jnp.ones((1,), bool), entries >= 0])
    bias = jnp.repeat(jnp.where(live, 0.0, -jnp.inf).astype(jnp.float32), tile_rows)[None, :]
    odd = (lax.axis_index("seq") % 2).astype(jnp.int32)[None]
    chunk = features // CHUNKS
    pieces = []
    fetched = None
    for c in range(CHUNKS):
        cols = slice(c * chunk, (c + 1) * chunk)
        stacked = jnp.stack([k_norm[:, cols], value_rows[:, cols]])
        if fetched is not None:
            stacked, _ = lax.optimization_barrier((stacked, fetched))
        fetched = fetch_neighbours(stacked, "seq")
        q_grad_c, k_grad_c, v_sum_c, *far = attention(
            odd, bias, q_norm, k_norm, value_rows, grad_rows, fetched, c * chunk // (HEADS_PER_STEP * HEAD)
        )
        for back in return_parts(far, "seq"):
            k_grad_c = k_grad_c + back[0].astype(jnp.float32)
            v_sum_c = v_sum_c + back[1].astype(jnp.float32)
        pieces.append((q_grad_c, k_grad_c, v_sum_c))
    q_norm_grad, k_norm_grad, v_sum = (
        jnp.concatenate([p[i] for p in pieces], axis=1) for i in range(3)
    )
    q_back, q_part = norm_backward(q_norm_grad, q_gain, q_hat, q_inv)
    k_back, k_part = norm_backward(k_norm_grad, k_gain, k_hat, k_inv)
    gain_grads = all_sum(jnp.concatenate([q_part, k_part]), ("dp", "seq"))
    q_gain_grad, k_gain_grad = gain_grads[:features], gain_grads[features:]
    return (
        q_back.astype(jnp.bfloat16)[None],
        k_back.astype(jnp.bfloat16)[None],
        v_sum.astype(jnp.bfloat16)[None],
        q_gain_grad,
        k_gain_grad,
    )


def solution(mesh):
    return jax.shard_map(
        body,
        mesh=mesh,
        in_specs=(
            P("dp", "seq", None),
            P("dp", "seq", None),
            P("dp", "seq", None),
            P("dp", "seq", None),
            P(),
            P(),
            P("seq", None),
        ),
        out_specs=(P("dp", "seq", None), P("dp", "seq", None), P("dp", "seq", None), P(), P()),
        check_vma=False,
    )
```

```python
import functools
import math

import jax
import jax.numpy as jnp
from jax import lax
from jax.experimental import pallas as pl
from jax.experimental.pallas import tpu as pltpu
from jax.sharding import PartitionSpec as P

HEAD = 128
LEVELS = 2
HEADS_PER_STEP = 4
CHUNK_HEADS = (12, 8)


EPS = 1e-06

NT = (((1,), (1,)), ((), ()))
TN = (((0,), (0,)), ((), ()))


def from_behind(value, axis, steps):
    count = lax.axis_size(axis)
    first, last = (max(0, -steps), min(count, count - steps))
    return lax.ppermute(value, axis, [(source, source + steps) for source in range(first, last)])


def pairs_permute(value, axis, pairs):
    count = lax.axis_size(axis)
    return lax.ppermute(value, axis, [(i, j) for i, j in pairs if 0 <= j < count])


def fetch_neighbours(value, axis):
    count = lax.axis_size(axis)
    behind = from_behind(value, axis, 1)
    ahead = from_behind(value, axis, -1)
    two = [(i, i + 2) for i in range(0, count, 2)] + [(i, i - 2) for i in range(1, count, 2)]
    far2 = pairs_permute(value, axis, two)
    odd = lax.axis_index(axis) % 2 == 1
    relay = pairs_permute(jnp.where(odd, ahead, behind), axis, [(i, i ^ 1) for i in range(count)])
    return [behind, ahead, far2, relay]


def return_parts(far, axis):
    count = lax.axis_size(axis)
    behind, ahead, for_partner, direct = far
    odd = lax.axis_index(axis) % 2 == 1
    swapped = pairs_permute(for_partner, axis, [(i, i ^ 1) for i in range(count)])

    def joined(own):
        return (own.astype(jnp.float32) + swapped.astype(jnp.float32)).astype(jnp.bfloat16)

    to_next = from_behind(jnp.where(odd, joined(ahead), ahead), axis, 1)
    to_previous = from_behind(jnp.where(odd, behind, joined(behind)), axis, -1)
    two = [(i, i + 2) for i in range(1, count, 2)] + [(i, i - 2) for i in range(0, count, 2)]
    return [to_next, to_previous, pairs_permute(direct, axis, two)]


def all_sum(value, axes):
    for axis in axes:
        count = lax.axis_size(axis)
        bit = 1
        while bit < count:
            value = value + lax.ppermute(value, axis, [(i, i ^ bit) for i in range(count)])
            bit *= 2
    return value


def level_offsets(levels):
    return [sign * 2**level for level in range(levels) for sign in (-1, 1)]


def normalize(raw):
    numbers = raw.astype(jnp.float32)
    inverse = lax.rsqrt(jnp.mean(numbers * numbers, axis=-1, keepdims=True) + EPS)
    return (numbers * inverse, inverse)


def norm_backward(grad_norm, gain, hat, inverse):
    scaled = grad_norm * gain
    inner = jnp.mean(scaled * hat, axis=-1, keepdims=True)
    return (inverse * (scaled - hat * inner), jnp.sum(grad_norm * hat, axis=0))


def attention_kernel(odd_ref, bias_ref, q_ref, k_ref, v_ref, g_ref, *refs):
    behind, ahead, far2, relay = refs[:4]
    dq_ref, dk_ref, dv_ref = refs[4:7]
    far = refs[7:]
    slots = len(far)
    rows = q_ref.shape[0]
    scale = 1.0 / math.sqrt(HEAD)
    odd = odd_ref[0] == 1
    bias = bias_ref[...]
    for h in range(q_ref.shape[1] // HEAD):
        cols = pl.ds(h * HEAD, HEAD)

        def pick(which, cols=cols):
            return jnp.concatenate(
                [
                    behind[which, :, cols],
                    ahead[which, :, cols],
                    jnp.where(odd, relay[which, :, cols], far2[which, :, cols]),
                    jnp.where(odd, far2[which, :, cols], relay[which, :, cols]),
                ],
                axis=0,
            )

        q = q_ref[:, cols]
        g = g_ref[:, cols]
        keys = jnp.concatenate([k_ref[:, cols], pick(0)], axis=0)
        vals = jnp.concatenate([v_ref[:, cols], pick(1)], axis=0)
        scores = lax.dot_general(q, keys, NT, preferred_element_type=jnp.float32) * scale + bias
        highest = jnp.max(scores, axis=1, keepdims=True)
        total = jnp.sum(jnp.exp(scores - highest), axis=1, keepdims=True)
        log_total = highest + jnp.log(total)
        prob = jnp.exp(scores - log_total).astype(jnp.bfloat16)
        attended = jnp.dot(prob, vals, preferred_element_type=jnp.float32)
        delta = jnp.sum(g.astype(jnp.float32) * attended, axis=1, keepdims=True)
        prob_grad = lax.dot_general(g, vals, NT, preferred_element_type=jnp.float32)
        score_grad = (prob.astype(jnp.float32) * (prob_grad - delta) * scale).astype(jnp.bfloat16)
        dq_ref[:, cols] = jnp.dot(score_grad, keys, preferred_element_type=jnp.float32)
        grad_k = lax.dot_general(score_grad, q, TN, preferred_element_type=jnp.float32)
        grad_v = lax.dot_general(prob, g, TN, preferred_element_type=jnp.float32)
        dk_ref[:, cols] = grad_k[:rows]
        dv_ref[:, cols] = grad_v[:rows]
        parts = [
            (grad_k[(slot + 1) * rows:(slot + 2) * rows].astype(jnp.bfloat16),
             grad_v[(slot + 1) * rows:(slot + 2) * rows].astype(jnp.bfloat16))
            for slot in range(slots)
        ]
        arranged = [
            parts[0],
            parts[1],
            tuple(jnp.where(odd, a, b) for a, b in zip(parts[2], parts[3])),
            tuple(jnp.where(odd, b, a) for a, b in zip(parts[2], parts[3])),
        ]
        for slot, (part_k, part_v) in enumerate(arranged):
            far[slot][0, :, cols] = part_k
            far[slot][1, :, cols] = part_v


def attention(odd, bias, q_norm, k_norm, value_rows, grad_rows, fetched, first=0):
    rows = q_norm.shape[0]
    features = fetched[0].shape[2]
    width = HEADS_PER_STEP * HEAD
    slots = 4
    own = pl.BlockSpec((rows, width), lambda h, odd: (0, h + first))
    tile = pl.BlockSpec((rows, width), lambda h, odd: (0, h))
    pair = pl.BlockSpec((2, rows, width), lambda h, odd: (0, 0, h))
    f32 = jax.ShapeDtypeStruct((rows, features), jnp.float32)
    bf16_pair = jax.ShapeDtypeStruct((2, rows, features), jnp.bfloat16)
    keys = rows * (slots + 1)
    flops = 2 * rows * keys * features * 6
    grid_spec = pltpu.PrefetchScalarGridSpec(
        num_scalar_prefetch=1,
        grid=(features // width,),
        in_specs=[pl.BlockSpec(bias.shape, lambda h, odd: (0, 0))] + [own] * 4 + [pair] * len(fetched),
        out_specs=[tile] * 3 + [pair] * slots,
    )
    return pl.pallas_call(
        attention_kernel,
        grid_spec=grid_spec,
        out_shape=[f32] * 3 + [bf16_pair] * slots,
        cost_estimate=pl.CostEstimate(
            flops=flops,
            transcendentals=2 * rows * keys * (features // HEAD),
            bytes_accessed=2 * rows * features * (4 + 2 * len(fetched)) + 12 * rows * features,
        ),
    )(odd, bias, q_norm, k_norm, value_rows, grad_rows, *fetched)


def body(q_raw, k_raw, values, cotangent, q_gain, k_gain, key_tiles):
    tile_rows = q_raw.shape[1]
    features = q_raw.shape[2]
    offsets = level_offsets(LEVELS)
    q_hat, q_inv = normalize(q_raw[0])
    k_hat, k_inv = normalize(k_raw[0])
    q_norm = (q_hat * q_gain).astype(jnp.bfloat16)
    k_norm = (k_hat * k_gain).astype(jnp.bfloat16)
    value_rows = values[0]
    grad_rows = cotangent[0]
    entries = key_tiles[0]
    live = jnp.concatenate([jnp.ones((1,), bool), entries >= 0])
    bias = jnp.repeat(jnp.where(live, 0.0, -jnp.inf).astype(jnp.float32), tile_rows)[None, :]
    odd = (lax.axis_index("seq") % 2).astype(jnp.int32)[None]
    pieces = []
    fetched = None
    start = 0
    for heads in CHUNK_HEADS:
        cols = slice(start, start + heads * HEAD)
        stacked = jnp.stack([k_norm[:, cols], value_rows[:, cols]])
        if fetched is not None:
            stacked, _ = lax.optimization_barrier((stacked, fetched))
        fetched = fetch_neighbours(stacked, "seq")
        q_grad_c, k_grad_c, v_sum_c, *far = attention(
            odd, bias, q_norm, k_norm, value_rows, grad_rows, fetched, start // (HEADS_PER_STEP * HEAD)
        )
        start += heads * HEAD
        for back in return_parts(far, "seq"):
            k_grad_c = k_grad_c + back[0].astype(jnp.float32)
            v_sum_c = v_sum_c + back[1].astype(jnp.float32)
        pieces.append((q_grad_c, k_grad_c, v_sum_c))
    q_norm_grad, k_norm_grad, v_sum = (
        jnp.concatenate([p[i] for p in pieces], axis=1) for i in range(3)
    )
    q_back, q_part = norm_backward(q_norm_grad, q_gain, q_hat, q_inv)
    k_back, k_part = norm_backward(k_norm_grad, k_gain, k_hat, k_inv)
    gain_grads = all_sum(jnp.concatenate([q_part, k_part]), ("dp", "seq"))
    q_gain_grad, k_gain_grad = gain_grads[:features], gain_grads[features:]
    return (
        q_back.astype(jnp.bfloat16)[None],
        k_back.astype(jnp.bfloat16)[None],
        v_sum.astype(jnp.bfloat16)[None],
        q_gain_grad,
        k_gain_grad,
    )


def solution(mesh):
    return jax.shard_map(
        body,
        mesh=mesh,
        in_specs=(
            P("dp", "seq", None),
            P("dp", "seq", None),
            P("dp", "seq", None),
            P("dp", "seq", None),
            P(),
            P(),
            P("seq", None),
        ),
        out_specs=(P("dp", "seq", None), P("dp", "seq", None), P("dp", "seq", None), P(), P()),
        check_vma=False,
    )
```

```python
import functools
import math

import jax
import jax.numpy as jnp
from jax import lax
from jax.experimental import pallas as pl
from jax.experimental.pallas import tpu as pltpu
from jax.sharding import PartitionSpec as P

HEAD = 128
LEVELS = 2
HEADS_PER_STEP = 2
CHUNK_HEADS = (14, 6)


EPS = 1e-06

NT = (((1,), (1,)), ((), ()))
TN = (((0,), (0,)), ((), ()))


def from_behind(value, axis, steps):
    count = lax.axis_size(axis)
    first, last = (max(0, -steps), min(count, count - steps))
    return lax.ppermute(value, axis, [(source, source + steps) for source in range(first, last)])


def pairs_permute(value, axis, pairs):
    count = lax.axis_size(axis)
    return lax.ppermute(value, axis, [(i, j) for i, j in pairs if 0 <= j < count])


def fetch_neighbours(value, axis):
    count = lax.axis_size(axis)
    behind = from_behind(value, axis, 1)
    ahead = from_behind(value, axis, -1)
    two = [(i, i + 2) for i in range(0, count, 2)] + [(i, i - 2) for i in range(1, count, 2)]
    far2 = pairs_permute(value, axis, two)
    odd = lax.axis_index(axis) % 2 == 1
    relay = pairs_permute(jnp.where(odd, ahead, behind), axis, [(i, i ^ 1) for i in range(count)])
    return [behind, ahead, far2, relay]


def return_parts(far, axis):
    count = lax.axis_size(axis)
    behind, ahead, for_partner, direct = far
    odd = lax.axis_index(axis) % 2 == 1
    swapped = pairs_permute(for_partner, axis, [(i, i ^ 1) for i in range(count)])

    def joined(own):
        return (own.astype(jnp.float32) + swapped.astype(jnp.float32)).astype(jnp.bfloat16)

    to_next = from_behind(jnp.where(odd, joined(ahead), ahead), axis, 1)
    to_previous = from_behind(jnp.where(odd, behind, joined(behind)), axis, -1)
    two = [(i, i + 2) for i in range(1, count, 2)] + [(i, i - 2) for i in range(0, count, 2)]
    return [to_next, to_previous, pairs_permute(direct, axis, two)]


def all_sum(value, axes):
    for axis in axes:
        count = lax.axis_size(axis)
        bit = 1
        while bit < count:
            value = value + lax.ppermute(value, axis, [(i, i ^ bit) for i in range(count)])
            bit *= 2
    return value


def level_offsets(levels):
    return [sign * 2**level for level in range(levels) for sign in (-1, 1)]


def normalize(raw):
    numbers = raw.astype(jnp.float32)
    inverse = lax.rsqrt(jnp.mean(numbers * numbers, axis=-1, keepdims=True) + EPS)
    return (numbers * inverse, inverse)


def norm_backward(grad_norm, gain, hat, inverse):
    scaled = grad_norm * gain
    inner = jnp.mean(scaled * hat, axis=-1, keepdims=True)
    return (inverse * (scaled - hat * inner), jnp.sum(grad_norm * hat, axis=0))


def attention_kernel(odd_ref, bias_ref, q_ref, k_ref, v_ref, g_ref, *refs):
    behind, ahead, far2, relay = refs[:4]
    dq_ref, dk_ref, dv_ref = refs[4:7]
    far = refs[7:]
    slots = len(far)
    rows = q_ref.shape[0]
    scale = 1.0 / math.sqrt(HEAD)
    odd = odd_ref[0] == 1
    bias = bias_ref[...]
    for h in range(q_ref.shape[1] // HEAD):
        cols = pl.ds(h * HEAD, HEAD)

        def pick(which, cols=cols):
            return jnp.concatenate(
                [
                    behind[which, :, cols],
                    ahead[which, :, cols],
                    jnp.where(odd, relay[which, :, cols], far2[which, :, cols]),
                    jnp.where(odd, far2[which, :, cols], relay[which, :, cols]),
                ],
                axis=0,
            )

        q = q_ref[:, cols]
        g = g_ref[:, cols]
        keys = jnp.concatenate([k_ref[:, cols], pick(0)], axis=0)
        vals = jnp.concatenate([v_ref[:, cols], pick(1)], axis=0)
        scores = lax.dot_general(q, keys, NT, preferred_element_type=jnp.float32) * scale + bias
        highest = jnp.max(scores, axis=1, keepdims=True)
        total = jnp.sum(jnp.exp(scores - highest), axis=1, keepdims=True)
        log_total = highest + jnp.log(total)
        prob = jnp.exp(scores - log_total).astype(jnp.bfloat16)
        attended = jnp.dot(prob, vals, preferred_element_type=jnp.float32)
        delta = jnp.sum(g.astype(jnp.float32) * attended, axis=1, keepdims=True)
        prob_grad = lax.dot_general(g, vals, NT, preferred_element_type=jnp.float32)
        score_grad = (prob.astype(jnp.float32) * (prob_grad - delta) * scale).astype(jnp.bfloat16)
        dq_ref[:, cols] = jnp.dot(score_grad, keys, preferred_element_type=jnp.float32)
        grad_k = lax.dot_general(score_grad, q, TN, preferred_element_type=jnp.float32)
        grad_v = lax.dot_general(prob, g, TN, preferred_element_type=jnp.float32)
        dk_ref[:, cols] = grad_k[:rows]
        dv_ref[:, cols] = grad_v[:rows]
        parts = [
            (grad_k[(slot + 1) * rows:(slot + 2) * rows].astype(jnp.bfloat16),
             grad_v[(slot + 1) * rows:(slot + 2) * rows].astype(jnp.bfloat16))
            for slot in range(slots)
        ]
        arranged = [
            parts[0],
            parts[1],
            tuple(jnp.where(odd, a, b) for a, b in zip(parts[2], parts[3])),
            tuple(jnp.where(odd, b, a) for a, b in zip(parts[2], parts[3])),
        ]
        for slot, (part_k, part_v) in enumerate(arranged):
            far[slot][0, :, cols] = part_k
            far[slot][1, :, cols] = part_v


def attention(odd, bias, q_norm, k_norm, value_rows, grad_rows, fetched, first=0):
    rows = q_norm.shape[0]
    features = fetched[0].shape[2]
    width = HEADS_PER_STEP * HEAD
    slots = 4
    own = pl.BlockSpec((rows, width), lambda h, odd: (0, h + first))
    tile = pl.BlockSpec((rows, width), lambda h, odd: (0, h))
    pair = pl.BlockSpec((2, rows, width), lambda h, odd: (0, 0, h))
    f32 = jax.ShapeDtypeStruct((rows, features), jnp.float32)
    bf16_pair = jax.ShapeDtypeStruct((2, rows, features), jnp.bfloat16)
    keys = rows * (slots + 1)
    flops = 2 * rows * keys * features * 6
    grid_spec = pltpu.PrefetchScalarGridSpec(
        num_scalar_prefetch=1,
        grid=(features // width,),
        in_specs=[pl.BlockSpec(bias.shape, lambda h, odd: (0, 0))] + [own] * 4 + [pair] * len(fetched),
        out_specs=[tile] * 3 + [pair] * slots,
    )
    return pl.pallas_call(
        attention_kernel,
        grid_spec=grid_spec,
        out_shape=[f32] * 3 + [bf16_pair] * slots,
        cost_estimate=pl.CostEstimate(
            flops=flops,
            transcendentals=2 * rows * keys * (features // HEAD),
            bytes_accessed=2 * rows * features * (4 + 2 * len(fetched)) + 12 * rows * features,
        ),
    )(odd, bias, q_norm, k_norm, value_rows, grad_rows, *fetched)


def body(q_raw, k_raw, values, cotangent, q_gain, k_gain, key_tiles):
    tile_rows = q_raw.shape[1]
    features = q_raw.shape[2]
    offsets = level_offsets(LEVELS)
    q_hat, q_inv = normalize(q_raw[0])
    k_hat, k_inv = normalize(k_raw[0])
    q_norm = (q_hat * q_gain).astype(jnp.bfloat16)
    k_norm = (k_hat * k_gain).astype(jnp.bfloat16)
    value_rows = values[0]
    grad_rows = cotangent[0]
    entries = key_tiles[0]
    live = jnp.concatenate([jnp.ones((1,), bool), entries >= 0])
    bias = jnp.repeat(jnp.where(live, 0.0, -jnp.inf).astype(jnp.float32), tile_rows)[None, :]
    odd = (lax.axis_index("seq") % 2).astype(jnp.int32)[None]
    pieces = []
    fetched = None
    start = 0
    for heads in CHUNK_HEADS:
        cols = slice(start, start + heads * HEAD)
        stacked = jnp.stack([k_norm[:, cols], value_rows[:, cols]])
        if fetched is not None:
            stacked, _ = lax.optimization_barrier((stacked, fetched))
        fetched = fetch_neighbours(stacked, "seq")
        q_grad_c, k_grad_c, v_sum_c, *far = attention(
            odd, bias, q_norm, k_norm, value_rows, grad_rows, fetched, start // (HEADS_PER_STEP * HEAD)
        )
        start += heads * HEAD
        for back in return_parts(far, "seq"):
            k_grad_c = k_grad_c + back[0].astype(jnp.float32)
            v_sum_c = v_sum_c + back[1].astype(jnp.float32)
        pieces.append((q_grad_c, k_grad_c, v_sum_c))
    q_norm_grad, k_norm_grad, v_sum = (
        jnp.concatenate([p[i] for p in pieces], axis=1) for i in range(3)
    )
    q_back, q_part = norm_backward(q_norm_grad, q_gain, q_hat, q_inv)
    k_back, k_part = norm_backward(k_norm_grad, k_gain, k_hat, k_inv)
    gain_grads = all_sum(jnp.concatenate([q_part, k_part]), ("dp", "seq"))
    q_gain_grad, k_gain_grad = gain_grads[:features], gain_grads[features:]
    return (
        q_back.astype(jnp.bfloat16)[None],
        k_back.astype(jnp.bfloat16)[None],
        v_sum.astype(jnp.bfloat16)[None],
        q_gain_grad,
        k_gain_grad,
    )


def solution(mesh):
    return jax.shard_map(
        body,
        mesh=mesh,
        in_specs=(
            P("dp", "seq", None),
            P("dp", "seq", None),
            P("dp", "seq", None),
            P("dp", "seq", None),
            P(),
            P(),
            P("seq", None),
        ),
        out_specs=(P("dp", "seq", None), P("dp", "seq", None), P("dp", "seq", None), P(), P()),
        check_vma=False,
    )
```

```python
import functools
import math

import jax
import jax.numpy as jnp
from jax import lax
from jax.experimental import pallas as pl
from jax.experimental.pallas import tpu as pltpu
from jax.sharding import PartitionSpec as P

HEAD = 128
LEVELS = 2
HEADS_PER_STEP = 4
CHUNK_HEADS = (12, 8)


EPS = 1e-06

NT = (((1,), (1,)), ((), ()))
TN = (((0,), (0,)), ((), ()))


def from_behind(value, axis, steps):
    count = lax.axis_size(axis)
    first, last = (max(0, -steps), min(count, count - steps))
    return lax.ppermute(value, axis, [(source, source + steps) for source in range(first, last)])


def pairs_permute(value, axis, pairs):
    count = lax.axis_size(axis)
    return lax.ppermute(value, axis, [(i, j) for i, j in pairs if 0 <= j < count])


def fetch_neighbours(value, axis):
    count = lax.axis_size(axis)
    behind = from_behind(value, axis, 1)
    ahead = from_behind(value, axis, -1)
    two = [(i, i + 2) for i in range(0, count, 2)] + [(i, i - 2) for i in range(1, count, 2)]
    far2 = pairs_permute(value, axis, two)
    odd = lax.axis_index(axis) % 2 == 1
    relay = pairs_permute(jnp.where(odd, ahead, behind), axis, [(i, i ^ 1) for i in range(count)])
    return [behind, ahead, far2, relay]


def return_parts(far, axis):
    count = lax.axis_size(axis)
    behind, ahead, for_partner, direct = far
    odd = lax.axis_index(axis) % 2 == 1
    swapped = pairs_permute(for_partner, axis, [(i, i ^ 1) for i in range(count)])

    def joined(own):
        return (own.astype(jnp.float32) + swapped.astype(jnp.float32)).astype(jnp.bfloat16)

    to_next = from_behind(jnp.where(odd, joined(ahead), ahead), axis, 1)
    to_previous = from_behind(jnp.where(odd, behind, joined(behind)), axis, -1)
    two = [(i, i + 2) for i in range(1, count, 2)] + [(i, i - 2) for i in range(0, count, 2)]
    return [to_next, to_previous, pairs_permute(direct, axis, two)]


def all_sum(value, axes):
    for axis in axes:
        count = lax.axis_size(axis)
        bit = 1
        while bit < count:
            value = value + lax.ppermute(value, axis, [(i, i ^ bit) for i in range(count)])
            bit *= 2
    return value


def level_offsets(levels):
    return [sign * 2**level for level in range(levels) for sign in (-1, 1)]


def normalize(raw):
    numbers = raw.astype(jnp.float32)
    inverse = lax.rsqrt(jnp.mean(numbers * numbers, axis=-1, keepdims=True) + EPS)
    return (numbers * inverse, inverse)


def norm_backward(grad_norm, gain, hat, inverse):
    scaled = grad_norm * gain
    inner = jnp.mean(scaled * hat, axis=-1, keepdims=True)
    return (inverse * (scaled - hat * inner), jnp.sum(grad_norm * hat, axis=0))


def attention_kernel(odd_ref, bias_ref, q_ref, k_ref, v_ref, g_ref, *refs):
    behind, ahead, far2, relay = refs[:4]
    dq_ref, dk_ref, dv_ref = refs[4:7]
    far = refs[7:]
    slots = len(far)
    rows = q_ref.shape[0]
    scale = 1.0 / math.sqrt(HEAD)
    odd = odd_ref[0] == 1
    bias = bias_ref[...]
    for h in range(q_ref.shape[1] // HEAD):
        cols = pl.ds(h * HEAD, HEAD)

        def pick(which, cols=cols):
            return jnp.concatenate(
                [
                    behind[which, :, cols],
                    ahead[which, :, cols],
                    jnp.where(odd, relay[which, :, cols], far2[which, :, cols]),
                    jnp.where(odd, far2[which, :, cols], relay[which, :, cols]),
                ],
                axis=0,
            )

        q = q_ref[:, cols]
        g = g_ref[:, cols]
        keys = jnp.concatenate([k_ref[:, cols], pick(0)], axis=0)
        vals = jnp.concatenate([v_ref[:, cols], pick(1)], axis=0)
        scores = lax.dot_general(q, keys, NT, preferred_element_type=jnp.float32) * scale + bias
        highest = jnp.max(scores, axis=1, keepdims=True)
        total = jnp.sum(jnp.exp(scores - highest), axis=1, keepdims=True)
        log_total = highest + jnp.log(total)
        prob = jnp.exp(scores - log_total).astype(jnp.bfloat16)
        attended = jnp.dot(prob, vals, preferred_element_type=jnp.float32)
        delta = jnp.sum(g.astype(jnp.float32) * attended, axis=1, keepdims=True)
        prob_grad = lax.dot_general(g, vals, NT, preferred_element_type=jnp.float32)
        score_grad = (prob.astype(jnp.float32) * (prob_grad - delta) * scale).astype(jnp.bfloat16)
        dq_ref[:, cols] = jnp.dot(score_grad, keys, preferred_element_type=jnp.float32)
        grad_k = lax.dot_general(score_grad, q, TN, preferred_element_type=jnp.float32)
        grad_v = lax.dot_general(prob, g, TN, preferred_element_type=jnp.float32)
        dk_ref[:, cols] = grad_k[:rows]
        dv_ref[:, cols] = grad_v[:rows]
        parts = [
            (grad_k[(slot + 1) * rows:(slot + 2) * rows].astype(jnp.bfloat16),
             grad_v[(slot + 1) * rows:(slot + 2) * rows].astype(jnp.bfloat16))
            for slot in range(slots)
        ]
        arranged = [
            parts[0],
            parts[1],
            tuple(jnp.where(odd, a, b) for a, b in zip(parts[2], parts[3])),
            tuple(jnp.where(odd, b, a) for a, b in zip(parts[2], parts[3])),
        ]
        for slot, (part_k, part_v) in enumerate(arranged):
            far[slot][0, :, cols] = part_k
            far[slot][1, :, cols] = part_v


def attention(odd, bias, q_norm, k_norm, value_rows, grad_rows, fetched, first=0):
    rows = q_norm.shape[0]
    features = fetched[0].shape[2]
    width = HEADS_PER_STEP * HEAD
    slots = 4
    own = pl.BlockSpec((rows, width), lambda h, odd: (0, h + first))
    tile = pl.BlockSpec((rows, width), lambda h, odd: (0, h))
    pair = pl.BlockSpec((2, rows, width), lambda h, odd: (0, 0, h))
    f32 = jax.ShapeDtypeStruct((rows, features), jnp.float32)
    bf16_pair = jax.ShapeDtypeStruct((2, rows, features), jnp.bfloat16)
    keys = rows * (slots + 1)
    flops = 2 * rows * keys * features * 6
    grid_spec = pltpu.PrefetchScalarGridSpec(
        num_scalar_prefetch=1,
        grid=(features // width,),
        in_specs=[pl.BlockSpec(bias.shape, lambda h, odd: (0, 0))] + [own] * 4 + [pair] * len(fetched),
        out_specs=[tile] * 3 + [pair] * slots,
    )
    return pl.pallas_call(
        attention_kernel,
        grid_spec=grid_spec,
        out_shape=[f32] * 3 + [bf16_pair] * slots,
        cost_estimate=pl.CostEstimate(
            flops=flops,
            transcendentals=2 * rows * keys * (features // HEAD),
            bytes_accessed=2 * rows * features * (4 + 2 * len(fetched)) + 12 * rows * features,
        ),
    )(odd, bias, q_norm, k_norm, value_rows, grad_rows, *fetched)


def body(q_raw, k_raw, values, cotangent, q_gain, k_gain, key_tiles):
    tile_rows = q_raw.shape[1]
    features = q_raw.shape[2]
    offsets = level_offsets(LEVELS)
    k_hat, k_inv = normalize(k_raw[0])
    k_norm = (k_hat * k_gain).astype(jnp.bfloat16)
    value_rows = values[0]
    grad_rows = cotangent[0]
    entries = key_tiles[0]
    live = jnp.concatenate([jnp.ones((1,), bool), entries >= 0])
    bias = jnp.repeat(jnp.where(live, 0.0, -jnp.inf).astype(jnp.float32), tile_rows)[None, :]
    odd = (lax.axis_index("seq") % 2).astype(jnp.int32)[None]
    pieces = []
    fetched = None
    start = 0
    for heads in CHUNK_HEADS:
        cols = slice(start, start + heads * HEAD)
        stacked = jnp.stack([k_norm[:, cols], value_rows[:, cols]])
        if fetched is not None:
            stacked, _ = lax.optimization_barrier((stacked, fetched))
        fetched = fetch_neighbours(stacked, "seq")
        if start == 0:
            q_in, _ = lax.optimization_barrier((q_raw[0], fetched))
            q_hat, q_inv = normalize(q_in)
            q_norm = (q_hat * q_gain).astype(jnp.bfloat16)
        q_grad_c, k_grad_c, v_sum_c, *far = attention(
            odd, bias, q_norm, k_norm, value_rows, grad_rows, fetched, start // (HEADS_PER_STEP * HEAD)
        )
        start += heads * HEAD
        for back in return_parts(far, "seq"):
            k_grad_c = k_grad_c + back[0].astype(jnp.float32)
            v_sum_c = v_sum_c + back[1].astype(jnp.float32)
        pieces.append((q_grad_c, k_grad_c, v_sum_c))
    q_norm_grad, k_norm_grad, v_sum = (
        jnp.concatenate([p[i] for p in pieces], axis=1) for i in range(3)
    )
    q_back, q_part = norm_backward(q_norm_grad, q_gain, q_hat, q_inv)
    k_back, k_part = norm_backward(k_norm_grad, k_gain, k_hat, k_inv)
    gain_grads = all_sum(jnp.concatenate([q_part, k_part]), ("dp", "seq"))
    q_gain_grad, k_gain_grad = gain_grads[:features], gain_grads[features:]
    return (
        q_back.astype(jnp.bfloat16)[None],
        k_back.astype(jnp.bfloat16)[None],
        v_sum.astype(jnp.bfloat16)[None],
        q_gain_grad,
        k_gain_grad,
    )


def solution(mesh):
    return jax.shard_map(
        body,
        mesh=mesh,
        in_specs=(
            P("dp", "seq", None),
            P("dp", "seq", None),
            P("dp", "seq", None),
            P("dp", "seq", None),
            P(),
            P(),
            P("seq", None),
        ),
        out_specs=(P("dp", "seq", None), P("dp", "seq", None), P("dp", "seq", None), P(), P()),
        check_vma=False,
    )
```

```python
import functools
import math

import jax
import jax.numpy as jnp
from jax import lax
from jax.experimental import pallas as pl
from jax.experimental.pallas import tpu as pltpu
from jax.sharding import PartitionSpec as P

HEAD = 128
LEVELS = 2
HEADS_PER_STEP = 4
CHUNK_HEADS = (12, 8)


EPS = 1e-06

NT = (((1,), (1,)), ((), ()))
TN = (((0,), (0,)), ((), ()))


def from_behind(value, axis, steps):
    count = lax.axis_size(axis)
    first, last = (max(0, -steps), min(count, count - steps))
    return lax.ppermute(value, axis, [(source, source + steps) for source in range(first, last)])


def pairs_permute(value, axis, pairs):
    count = lax.axis_size(axis)
    return lax.ppermute(value, axis, [(i, j) for i, j in pairs if 0 <= j < count])


def fetch_neighbours(value, axis):
    count = lax.axis_size(axis)
    behind = from_behind(value, axis, 1)
    ahead = from_behind(value, axis, -1)
    two = [(i, i + 2) for i in range(0, count, 2)] + [(i, i - 2) for i in range(1, count, 2)]
    far2 = pairs_permute(value, axis, two)
    odd = lax.axis_index(axis) % 2 == 1
    relay = pairs_permute(jnp.where(odd, ahead, behind), axis, [(i, i ^ 1) for i in range(count)])
    return [behind, ahead, far2, relay]


def return_parts(far, axis):
    count = lax.axis_size(axis)
    behind, ahead, for_partner, direct = far
    odd = lax.axis_index(axis) % 2 == 1
    swapped = pairs_permute(for_partner, axis, [(i, i ^ 1) for i in range(count)])

    def joined(own):
        return (own.astype(jnp.float32) + swapped.astype(jnp.float32)).astype(jnp.bfloat16)

    to_next = from_behind(jnp.where(odd, joined(ahead), ahead), axis, 1)
    to_previous = from_behind(jnp.where(odd, behind, joined(behind)), axis, -1)
    two = [(i, i + 2) for i in range(1, count, 2)] + [(i, i - 2) for i in range(0, count, 2)]
    return [to_next, to_previous, pairs_permute(direct, axis, two)]


def all_sum(value, axes):
    for axis in axes:
        count = lax.axis_size(axis)
        bit = 1
        while bit < count:
            value = value + lax.ppermute(value, axis, [(i, i ^ bit) for i in range(count)])
            bit *= 2
    return value


def level_offsets(levels):
    return [sign * 2**level for level in range(levels) for sign in (-1, 1)]


def normalize(raw):
    numbers = raw.astype(jnp.float32)
    inverse = lax.rsqrt(jnp.mean(numbers * numbers, axis=-1, keepdims=True) + EPS)
    return (numbers * inverse, inverse)


def norm_backward(grad_norm, gain, hat, inverse):
    scaled = grad_norm * gain
    inner = jnp.mean(scaled * hat, axis=-1, keepdims=True)
    return (inverse * (scaled - hat * inner), jnp.sum(grad_norm * hat, axis=0))


def attention_kernel(odd_ref, bias_ref, q_ref, k_ref, v_ref, g_ref, *refs):
    behind, ahead, far2, relay = refs[:4]
    dq_ref, dk_ref, dv_ref = refs[4:7]
    far = refs[7:]
    slots = len(far)
    rows = q_ref.shape[0]
    scale = 1.0 / math.sqrt(HEAD)
    odd = odd_ref[0] == 1
    bias = bias_ref[...]
    for h in range(q_ref.shape[1] // HEAD):
        cols = pl.ds(h * HEAD, HEAD)

        def pick(which, cols=cols):
            return jnp.concatenate(
                [
                    behind[which, :, cols],
                    ahead[which, :, cols],
                    jnp.where(odd, relay[which, :, cols], far2[which, :, cols]),
                    jnp.where(odd, far2[which, :, cols], relay[which, :, cols]),
                ],
                axis=0,
            )

        q = q_ref[:, cols]
        g = g_ref[:, cols]
        keys = jnp.concatenate([k_ref[:, cols], pick(0)], axis=0)
        vals = jnp.concatenate([v_ref[:, cols], pick(1)], axis=0)
        scores = lax.dot_general(q, keys, NT, preferred_element_type=jnp.float32) * scale + bias
        highest = jnp.max(scores, axis=1, keepdims=True)
        shifted = jnp.exp(scores - highest)
        total = jnp.sum(shifted, axis=1, keepdims=True)
        prob = (shifted * (1.0 / total)).astype(jnp.bfloat16)
        attended = jnp.dot(prob, vals, preferred_element_type=jnp.float32)
        delta = jnp.sum(g.astype(jnp.float32) * attended, axis=1, keepdims=True)
        prob_grad = lax.dot_general(g, vals, NT, preferred_element_type=jnp.float32)
        score_grad = (prob.astype(jnp.float32) * (prob_grad - delta) * scale).astype(jnp.bfloat16)
        dq_ref[:, cols] = jnp.dot(score_grad, keys, preferred_element_type=jnp.float32)
        grad_k = lax.dot_general(score_grad, q, TN, preferred_element_type=jnp.float32)
        grad_v = lax.dot_general(prob, g, TN, preferred_element_type=jnp.float32)
        dk_ref[:, cols] = grad_k[:rows]
        dv_ref[:, cols] = grad_v[:rows]
        parts = [
            (grad_k[(slot + 1) * rows:(slot + 2) * rows].astype(jnp.bfloat16),
             grad_v[(slot + 1) * rows:(slot + 2) * rows].astype(jnp.bfloat16))
            for slot in range(slots)
        ]
        arranged = [
            parts[0],
            parts[1],
            tuple(jnp.where(odd, a, b) for a, b in zip(parts[2], parts[3])),
            tuple(jnp.where(odd, b, a) for a, b in zip(parts[2], parts[3])),
        ]
        for slot, (part_k, part_v) in enumerate(arranged):
            far[slot][0, :, cols] = part_k
            far[slot][1, :, cols] = part_v


def attention(odd, bias, q_norm, k_norm, value_rows, grad_rows, fetched, first=0):
    rows = q_norm.shape[0]
    features = fetched[0].shape[2]
    width = HEADS_PER_STEP * HEAD
    slots = 4
    own = pl.BlockSpec((rows, width), lambda h, odd: (0, h + first))
    tile = pl.BlockSpec((rows, width), lambda h, odd: (0, h))
    pair = pl.BlockSpec((2, rows, width), lambda h, odd: (0, 0, h))
    f32 = jax.ShapeDtypeStruct((rows, features), jnp.float32)
    bf16_pair = jax.ShapeDtypeStruct((2, rows, features), jnp.bfloat16)
    keys = rows * (slots + 1)
    flops = 2 * rows * keys * features * 6
    grid_spec = pltpu.PrefetchScalarGridSpec(
        num_scalar_prefetch=1,
        grid=(features // width,),
        in_specs=[pl.BlockSpec(bias.shape, lambda h, odd: (0, 0))] + [own] * 4 + [pair] * len(fetched),
        out_specs=[tile] * 3 + [pair] * slots,
    )
    return pl.pallas_call(
        attention_kernel,
        grid_spec=grid_spec,
        out_shape=[f32] * 3 + [bf16_pair] * slots,
        cost_estimate=pl.CostEstimate(
            flops=flops,
            transcendentals=2 * rows * keys * (features // HEAD),
            bytes_accessed=2 * rows * features * (4 + 2 * len(fetched)) + 12 * rows * features,
        ),
    )(odd, bias, q_norm, k_norm, value_rows, grad_rows, *fetched)


def body(q_raw, k_raw, values, cotangent, q_gain, k_gain, key_tiles):
    tile_rows = q_raw.shape[1]
    features = q_raw.shape[2]
    offsets = level_offsets(LEVELS)
    q_hat, q_inv = normalize(q_raw[0])
    k_hat, k_inv = normalize(k_raw[0])
    q_norm = (q_hat * q_gain).astype(jnp.bfloat16)
    k_norm = (k_hat * k_gain).astype(jnp.bfloat16)
    value_rows = values[0]
    grad_rows = cotangent[0]
    entries = key_tiles[0]
    live = jnp.concatenate([jnp.ones((1,), bool), entries >= 0])
    bias = jnp.repeat(jnp.where(live, 0.0, -jnp.inf).astype(jnp.float32), tile_rows)[None, :]
    odd = (lax.axis_index("seq") % 2).astype(jnp.int32)[None]
    pieces = []
    fetched = None
    start = 0
    for heads in CHUNK_HEADS:
        cols = slice(start, start + heads * HEAD)
        stacked = jnp.stack([k_norm[:, cols], value_rows[:, cols]])
        if fetched is not None:
            stacked, _ = lax.optimization_barrier((stacked, fetched))
        fetched = fetch_neighbours(stacked, "seq")
        q_grad_c, k_grad_c, v_sum_c, *far = attention(
            odd, bias, q_norm, k_norm, value_rows, grad_rows, fetched, start // (HEADS_PER_STEP * HEAD)
        )
        start += heads * HEAD
        for back in return_parts(far, "seq"):
            k_grad_c = k_grad_c + back[0].astype(jnp.float32)
            v_sum_c = v_sum_c + back[1].astype(jnp.float32)
        pieces.append((q_grad_c, k_grad_c, v_sum_c))
    q_norm_grad, k_norm_grad, v_sum = (
        jnp.concatenate([p[i] for p in pieces], axis=1) for i in range(3)
    )
    q_back, q_part = norm_backward(q_norm_grad, q_gain, q_hat, q_inv)
    k_back, k_part = norm_backward(k_norm_grad, k_gain, k_hat, k_inv)
    gain_grads = all_sum(jnp.concatenate([q_part, k_part]), ("dp", "seq"))
    q_gain_grad, k_gain_grad = gain_grads[:features], gain_grads[features:]
    return (
        q_back.astype(jnp.bfloat16)[None],
        k_back.astype(jnp.bfloat16)[None],
        v_sum.astype(jnp.bfloat16)[None],
        q_gain_grad,
        k_gain_grad,
    )


def solution(mesh):
    return jax.shard_map(
        body,
        mesh=mesh,
        in_specs=(
            P("dp", "seq", None),
            P("dp", "seq", None),
            P("dp", "seq", None),
            P("dp", "seq", None),
            P(),
            P(),
            P("seq", None),
        ),
        out_specs=(P("dp", "seq", None), P("dp", "seq", None), P("dp", "seq", None), P(), P()),
        check_vma=False,
    )
```
